32 devices in a mesh: blk: 16 (over z, y, core), rhs: 2 (over x).
Axes of the slice: x: 2, y: 2, z: 4, core: 2. Of those that a mesh axis runs over, the one named last changes fastest.
Arguments:
- factor_panel: float32 [2, 1024, 16384], P(None, None, 'blk'), may hold values from -0.0625 to 0.0625
- solved_before: float32 [16384, 512], P('blk', 'rhs'), may hold values from -6 to 6
- right_side: float32 [2, 1024, 512], P(None, None, 'rhs'), may hold values from -6 to 6
- diag_inverse: float32 [2, 1024, 1024], P(None, 'blk', 'rhs'), may hold values from -0.2 to 1.5, as said below
- coupling: float32 [1024, 1024], P(None, 'blk'), may hold values from -0.25 to 0.25
Outputs:
- solved: float32 [2, 1024, 512], P(None, 'blk', 'rhs')
The draws below stay inside these ranges and needn't reach their ends.
Inputs may be any that keep to these rules, and one draw needn't show every extreme that they name: `diag_inverse`: each of the two blocks is lower triangular with a positive diagonal.
All inputs are finite; a program needn't handle non-finite values.
Results may differ from the reference program's by a relative error of at most 0.00009.
Values sent between devices are 32-bit elements; how exact they have to be, the bound alone decides.
No kernel may reach another device: no remote copies, remote signals or barrier semaphores. Data moves between devices by JAX's collectives and lax.ppermute only.
A program may use at most 64 MiB of HBM per device.

```python
import math
import jax
import jax.numpy as jnp
from jax import lax

NB = 1024
PREV = 16384
RHS = 512


def draw_diag_inverse(key, part):
    key_off, key_diag = jax.random.split(key)
    row_index = lax.broadcasted_iota(jnp.int32, (2, NB, NB), 1)
    col_index = lax.broadcasted_iota(jnp.int32, (2, NB, NB), 2)
    lower = jax.random.normal(key_off, (2, NB, NB), jnp.float32)
    lower = jnp.clip(lower * (0.8 / math.sqrt(NB)), -0.2, 0.2)
    diagonal = jax.random.uniform(key_diag, (2, NB, NB), jnp.float32, 0.5, 1.5)
    return jnp.where(col_index < row_index, lower, jnp.where(col_index == row_index, diagonal, 0.0))


def strengthened(result, stream_key, source, target, blocks, factor):
    def block_of(dim):
        return (jnp.arange(result.shape[dim]) // (result.shape[dim] // blocks)).reshape((-1,) + (1,) * (result.ndim - 1 - dim))

    first = jax.random.permutation(stream_key, blocks)[block_of(target)]
    far = (block_of(target) + blocks // 2) % blocks
    return jnp.where((block_of(source) == first) | (block_of(source) == far), factor * result, result)


def block_scale(stream_key, dims, cuts, smallest, largest):
    factor_of = 1.0
    for axis_at, shards_of in cuts:
        draws = jax.random.uniform(jax.random.fold_in(jax.random.fold_in(stream_key, 6), axis_at), (shards_of,), jnp.float32, smallest / len(cuts), largest / len(cuts))
        factor_of = factor_of * jnp.repeat(jnp.exp(draws), dims[axis_at] // shards_of).reshape((-1,) + (1,) * (len(dims) - 1 - axis_at))
    return factor_of


def centred(own_key, shape, width, most, shards=(), kind=jnp.bfloat16):
    entries = width * jax.random.normal(own_key, shape, jnp.float32)
    if shards:
        entries = entries * block_scale(own_key, shape, shards, -0.22, 0.18)
    return jnp.clip(entries, -most, most).astype(kind)


def noise_with(stream_key, extent, deviation, most, shards, heavy, held_as=jnp.bfloat16):
    array = deviation * jax.random.normal(stream_key, extent, jnp.float32)
    if shards:
        array = array * block_scale(stream_key, extent, shards, -0.22, 0.18)
    return jnp.clip(strengthened(array, jax.random.fold_in(stream_key, 3), *heavy), -most, most).astype(held_as)


def setup_inputs(seed: int = 0) -> dict:
    seeds = jax.random.split(jax.random.key(seed), 6)
    factor_panel = noise_with(seeds[0], (2, NB, PREV), PREV ** -0.5, 0.0625, ((2, 16),), (2, 1, 16, 2.0), jnp.float32)
    solved_before = centred(seeds[1], (PREV, RHS), 1.0, 6.0, ((0, 16), (1, 2)), jnp.float32)
    right_side = centred(seeds[2], (2, NB, RHS), 1.0, 6.0, ((2, 2),), jnp.float32)
    diag_inverse = draw_diag_inverse(jax.random.fold_in(seeds[5], 71), 0)
    coupling = noise_with(seeds[4], (NB, NB), NB ** -0.5, 0.25, ((1, 16),), (1, 0, 16, 2.0), jnp.float32)
    return {"factor_panel": factor_panel, "solved_before": solved_before, "right_side": right_side, "diag_inverse": diag_inverse, "coupling": coupling}


def product(left, right):
    return jnp.dot(left, right, precision=lax.Precision.HIGHEST, preferred_element_type=jnp.float32)


def reference(factor_panel, solved_before, right_side, diag_inverse, coupling):
    first_sum = product(factor_panel[0], solved_before)
    first_block = product(diag_inverse[0], right_side[0] - first_sum)
    second_sum = product(factor_panel[1], solved_before) + product(coupling, first_block)
    second_block = product(diag_inverse[1], right_side[1] - second_sum)
    return jnp.stack([first_block, second_block])
```

```python
import jax
import jax.numpy as jnp
from jax import lax
from jax.sharding import PartitionSpec as P


def product(left, right):
    return jnp.dot(left, right, precision=lax.Precision.HIGHEST, preferred_element_type=jnp.float32)


def halving_sum_scatter(x, axis, n):
    k = n.bit_length() - 1
    me = lax.axis_index(axis)
    rows = x.shape[0] // n
    y = x.reshape((2,) * k + (rows,) + x.shape[1:])
    for j in range(k):
        bit_axis = k - 1 - j
        mine = (me >> j) & 1
        keep = lax.dynamic_index_in_dim(y, mine, bit_axis, keepdims=False)
        send = lax.dynamic_index_in_dim(y, 1 - mine, bit_axis, keepdims=False)
        got = lax.ppermute(send, axis, [(i, i ^ (1 << j)) for i in range(n)])
        y = keep + got
    return y.reshape((rows,) + x.shape[1:])


def doubling_gather(x, axis, n):
    k = n.bit_length() - 1
    me = lax.axis_index(axis)
    y = x[None]
    for j in reversed(range(k)):
        mine = (me >> j) & 1
        got = lax.ppermute(y, axis, [(i, i ^ (1 << j)) for i in range(n)])
        low = jnp.where(mine == 0, y, got)
        high = jnp.where(mine == 0, got, y)
        y = jnp.stack([low, high], 1).reshape((-1,) + x.shape)
    return y.reshape((-1,) + x.shape[1:])


def make_shards(n):
    power_of_two = n > 1 and (n & (n - 1)) == 0

    def sum_scatter(x):
        if power_of_two:
            return halving_sum_scatter(x, "blk", n)
        return lax.psum_scatter(x, "blk", scatter_dimension=0, tiled=True)

    def gather(x):
        if power_of_two:
            return doubling_gather(x, "blk", n)
        return lax.all_gather(x, "blk", axis=0, tiled=True)

    def shards(factor_panel, solved_before, right_side, diag_inverse, coupling):
        inverse_full = lax.all_gather(diag_inverse, "rhs", axis=2, tiled=True)
        own_count = diag_inverse.shape[1]
        my_index = lax.axis_index("blk")

        def own_slice(matrix):
            return lax.dynamic_slice_in_dim(matrix, my_index * own_count, own_count, 0)

        first_part = sum_scatter(product(factor_panel[0], solved_before))
        first_remains = gather(own_slice(right_side[0]) - first_part)
        first_block = product(inverse_full[0], first_remains)
        second_part = sum_scatter(
            product(factor_panel[1], solved_before) + product(coupling, first_block)
        )
        second_remains = gather(own_slice(right_side[1]) - second_part)
        second_block = product(inverse_full[1], second_remains)
        return jnp.stack([first_block, second_block])

    return shards


def solution(mesh):
    placed = (
        P(None, None, "blk"),
        P("blk", "rhs"),
        P(None, None, "rhs"),
        P(None, "blk", "rhs"),
        P(None, "blk"),
    )
    return jax.shard_map(
        make_shards(mesh.shape["blk"]), mesh=mesh, in_specs=placed, out_specs=P(None, "blk", "rhs"), check_vma=False
    )
```

```python
import jax
import jax.numpy as jnp
from jax import lax
from jax.sharding import PartitionSpec as P


def product(left, right):
    return jnp.dot(left, right, precision=lax.Precision.HIGHEST, preferred_element_type=jnp.float32)


def halving_sum_scatter(x, axis, n):
    k = n.bit_length() - 1
    me = lax.axis_index(axis)
    rows = x.shape[0] // n
    y = x.reshape((2,) * k + (rows,) + x.shape[1:])
    for j in range(k):
        bit_axis = k - 1 - j
        mine = (me >> j) & 1
        keep = lax.dynamic_index_in_dim(y, mine, bit_axis, keepdims=False)
        send = lax.dynamic_index_in_dim(y, 1 - mine, bit_axis, keepdims=False)
        got = lax.ppermute(send, axis, [(i, i ^ (1 << j)) for i in range(n)])
        y = keep + got
    return y.reshape((rows,) + x.shape[1:])


def doubling_gather(x, axis, n):
    k = n.bit_length() - 1
    me = lax.axis_index(axis)
    y = x[None]
    for j in reversed(range(k)):
        mine = (me >> j) & 1
        got = lax.ppermute(y, axis, [(i, i ^ (1 << j)) for i in range(n)])
        low = jnp.where(mine == 0, y, got)
        high = jnp.where(mine == 0, got, y)
        y = jnp.stack([low, high], 1).reshape((-1,) + x.shape)
    return y.reshape((-1,) + x.shape[1:])


def make_shards(n, m):
    power_of_two = n > 1 and (n & (n - 1)) == 0
    rhs_power_of_two = m > 1 and (m & (m - 1)) == 0

    def sum_scatter(x):
        if power_of_two:
            return halving_sum_scatter(x, "blk", n)
        return lax.psum_scatter(x, "blk", scatter_dimension=0, tiled=True)

    def gather(x):
        if power_of_two:
            return doubling_gather(x, "blk", n)
        return lax.all_gather(x, "blk", axis=0, tiled=True)

    def shards(factor_panel, solved_before, right_side, diag_inverse, coupling):
        if rhs_power_of_two:
            pieces = doubling_gather(diag_inverse[None], "rhs", m)
            inverse_full = jnp.concatenate(list(pieces), axis=2)
        else:
            inverse_full = lax.all_gather(diag_inverse, "rhs", axis=2, tiled=True)
        own_count = diag_inverse.shape[1]
        my_index = lax.axis_index("blk")

        def own_slice(matrix):
            return lax.dynamic_slice_in_dim(matrix, my_index * own_count, own_count, 0)

        rows = factor_panel.shape[1]
        both_sums = product(factor_panel.reshape(2 * rows, -1), solved_before)
        first_part = sum_scatter(both_sums[:rows])
        first_remains = gather(own_slice(right_side[0]) - first_part)
        first_block = product(inverse_full[0], first_remains)
        second_part = sum_scatter(
            both_sums[rows:] + product(coupling, first_block)
        )
        second_remains = gather(own_slice(right_side[1]) - second_part)
        second_block = product(inverse_full[1], second_remains)
        return jnp.stack([first_block, second_block])

    return shards


def solution(mesh):
    placed = (
        P(None, None, "blk"),
        P("blk", "rhs"),
        P(None, None, "rhs"),
        P(None, "blk", "rhs"),
        P(None, "blk"),
    )
    return jax.shard_map(
        make_shards(mesh.shape["blk"], mesh.shape["rhs"]), mesh=mesh, in_specs=placed, out_specs=P(None, "blk", "rhs"), check_vma=False
    )
```

```python
import jax
import jax.numpy as jnp
from jax import lax
from jax.sharding import PartitionSpec as P


def product(left, right):
    return jnp.dot(left, right, precision=lax.Precision.HIGHEST, preferred_element_type=jnp.float32)


def halving_sum_scatter(x, axis, n, riders=None):
    k = n.bit_length() - 1
    me = lax.axis_index(axis)
    rows = x.shape[0] // n
    y = x.reshape((2,) * k + (rows,) + x.shape[1:])
    for j in range(k):
        bit_axis = k - 1 - j
        mine = (me >> j) & 1
        keep = lax.dynamic_index_in_dim(y, mine, bit_axis, keepdims=False)
        send = lax.dynamic_index_in_dim(y, 1 - mine, bit_axis, keepdims=False)
        got = lax.ppermute(send, axis, [(i, i ^ (1 << j)) for i in range(n)])
        if j == 1 and riders is not None:
            got, riders = lax.optimization_barrier((got, riders))
        y = keep + got
    return y.reshape((rows,) + x.shape[1:]), riders


def doubling_gather(x, axis, n):
    k = n.bit_length() - 1
    me = lax.axis_index(axis)
    y = x[None]
    for j in reversed(range(k)):
        mine = (me >> j) & 1
        got = lax.ppermute(y, axis, [(i, i ^ (1 << j)) for i in range(n)])
        low = jnp.where(mine == 0, y, got)
        high = jnp.where(mine == 0, got, y)
        y = jnp.stack([low, high], 1).reshape((-1,) + x.shape)
    return y.reshape((-1,) + x.shape[1:])


def make_shards(n, m):
    power_of_two = n > 1 and (n & (n - 1)) == 0
    rhs_power_of_two = m > 1 and (m & (m - 1)) == 0

    def sum_scatter(x, riders=None):
        if power_of_two and n >= 4:
            return halving_sum_scatter(x, "blk", n, riders)
        return lax.psum_scatter(x, "blk", scatter_dimension=0, tiled=True), riders

    def gather(x):
        if power_of_two:
            return doubling_gather(x, "blk", n)
        return lax.all_gather(x, "blk", axis=0, tiled=True)

    def shards(factor_panel, solved_before, right_side, diag_inverse, coupling):
        if rhs_power_of_two:
            inverse_pieces = doubling_gather(diag_inverse[None], "rhs", m)
        else:
            inverse_pieces = lax.all_gather(diag_inverse, "rhs", axis=0)
        own_count = diag_inverse.shape[1]
        my_index = lax.axis_index("blk")

        def own_slice(matrix):
            return lax.dynamic_slice_in_dim(matrix, my_index * own_count, own_count, 0)

        first_sum = product(factor_panel[0], solved_before)
        first_sum, inverse_pieces = lax.optimization_barrier((first_sum, inverse_pieces))
        inverse_full = jnp.concatenate(list(inverse_pieces), axis=2)
        panel_sum = product(factor_panel[1], solved_before)
        first_part, panel_sum = sum_scatter(first_sum, panel_sum)
        first_remains = gather(own_slice(right_side[0]) - first_part)
        first_block = product(inverse_full[0], first_remains)
        second_part, _ = sum_scatter(panel_sum + product(coupling, first_block))
        second_remains = gather(own_slice(right_side[1]) - second_part)
        second_block = product(inverse_full[1], second_remains)
        return jnp.stack([first_block, second_block])

    return shards


def solution(mesh):
    placed = (
        P(None, None, "blk"),
        P("blk", "rhs"),
        P(None, None, "rhs"),
        P(None, "blk", "rhs"),
        P(None, "blk"),
    )
    return jax.shard_map(
        make_shards(mesh.shape["blk"], mesh.shape["rhs"]), mesh=mesh, in_specs=placed, out_specs=P(None, "blk", "rhs"), check_vma=False
    )
```

```python
import jax
import jax.numpy as jnp
from jax import lax
from jax.sharding import PartitionSpec as P


def product(left, right):
    return jnp.dot(left, right, precision=lax.Precision.HIGHEST, preferred_element_type=jnp.float32)


def halving_sum_scatter(x, axis, n, riders=None):
    k = n.bit_length() - 1
    me = lax.axis_index(axis)
    rows = x.shape[0] // n
    y = x.reshape((2,) * k + (rows,) + x.shape[1:])
    for j in range(k):
        bit_axis = k - 1 - j
        mine = (me >> j) & 1
        keep = lax.dynamic_index_in_dim(y, mine, bit_axis, keepdims=False)
        send = lax.dynamic_index_in_dim(y, 1 - mine, bit_axis, keepdims=False)
        got = lax.ppermute(send, axis, [(i, i ^ (1 << j)) for i in range(n)])
        if j == 1 and riders is not None:
            got, riders = lax.optimization_barrier((got, riders))
        y = keep + got
    return y.reshape((rows,) + x.shape[1:]), riders


def doubling_gather(x, axis, n, stop=0):
    k = n.bit_length() - 1
    me = lax.axis_index(axis)
    y = x[None]
    for j in reversed(range(stop, k)):
        mine = (me >> j) & 1
        got = lax.ppermute(y, axis, [(i, i ^ (1 << j)) for i in range(n)])
        low = jnp.where(mine == 0, y, got)
        high = jnp.where(mine == 0, got, y)
        y = jnp.stack([low, high], 1).reshape((-1,) + x.shape)
    return y.reshape((-1,) + x.shape[1:])


def make_shards(n, m):
    power_of_two = n > 1 and (n & (n - 1)) == 0
    rhs_power_of_two = m > 1 and (m & (m - 1)) == 0

    def sum_scatter(x, riders=None):
        if power_of_two and n >= 4:
            return halving_sum_scatter(x, "blk", n, riders)
        return lax.psum_scatter(x, "blk", scatter_dimension=0, tiled=True), riders

    def gather(x):
        if power_of_two:
            return doubling_gather(x, "blk", n)
        return lax.all_gather(x, "blk", axis=0, tiled=True)

    def shards(factor_panel, solved_before, right_side, diag_inverse, coupling):
        own_count = diag_inverse.shape[1]
        my_index = lax.axis_index("blk")
        if power_of_two:
            partner_inverse = lax.ppermute(diag_inverse, "blk", [(i, i ^ 1) for i in range(n)])
            both_inverse = jnp.stack([diag_inverse, partner_inverse])
        else:
            both_inverse = diag_inverse[None]
        if rhs_power_of_two:
            inverse_pieces = doubling_gather(both_inverse[None], "rhs", m)
        else:
            inverse_pieces = lax.all_gather(both_inverse, "rhs", axis=0)

        def gather_apply(own_rows, mine_inverse, partner_rows_inverse):
            if not power_of_two:
                return product(mine_inverse, gather(own_rows))
            half = doubling_gather(own_rows, "blk", n, stop=1)
            core = my_index & 1

            def pick(matrix):
                split = matrix.reshape(matrix.shape[0], n // 2, 2, own_count)
                return lax.dynamic_index_in_dim(split, core, 2, keepdims=False).reshape(matrix.shape[0], -1)

            theirs = product(pick(partner_rows_inverse), half)
            return product(pick(mine_inverse), half) + lax.ppermute(theirs, "blk", [(i, i ^ 1) for i in range(n)])

        def own_slice(matrix):
            return lax.dynamic_slice_in_dim(matrix, my_index * own_count, own_count, 0)

        first_sum = product(factor_panel[0], solved_before)
        first_sum, inverse_pieces = lax.optimization_barrier((first_sum, inverse_pieces))
        inverse_full = jnp.concatenate(list(inverse_pieces), axis=3)
        partner_full = inverse_full[-1]
        panel_sum = product(factor_panel[1], solved_before)
        first_part, panel_sum = sum_scatter(first_sum, panel_sum)
        first_block = gather_apply(own_slice(right_side[0]) - first_part, inverse_full[0, 0], partner_full[0])
        second_part, _ = sum_scatter(panel_sum + product(coupling, first_block))
        second_block = gather_apply(own_slice(right_side[1]) - second_part, inverse_full[0, 1], partner_full[1])
        return jnp.stack([first_block, second_block])

    return shards


def solution(mesh):
    placed = (
        P(None, None, "blk"),
        P("blk", "rhs"),
        P(None, None, "rhs"),
        P(None, "blk", "rhs"),
        P(None, "blk"),
    )
    return jax.shard_map(
        make_shards(mesh.shape["blk"], mesh.shape["rhs"]), mesh=mesh, in_specs=placed, out_specs=P(None, "blk", "rhs"), check_vma=False
    )
```

```python
import jax
import jax.numpy as jnp
from jax import lax
from jax.sharding import PartitionSpec as P


def product(left, right):
    return jnp.dot(left, right, precision=lax.Precision.HIGHEST, preferred_element_type=jnp.float32)


def halving_sum_scatter(x, axis, n, riders=None):
    k = n.bit_length() - 1
    me = lax.axis_index(axis)
    rows = x.shape[0] // n
    y = x.reshape((2,) * k + (rows,) + x.shape[1:])
    for j in range(k):
        bit_axis = k - 1 - j
        mine = (me >> j) & 1
        keep = lax.dynamic_index_in_dim(y, mine, bit_axis, keepdims=False)
        send = lax.dynamic_index_in_dim(y, 1 - mine, bit_axis, keepdims=False)
        got = lax.ppermute(send, axis, [(i, i ^ (1 << j)) for i in range(n)])
        if j == 1 and riders is not None:
            got, riders = lax.optimization_barrier((got, riders))
        y = keep + got
    return y.reshape((rows,) + x.shape[1:]), riders


def doubling_gather(x, axis, n):
    k = n.bit_length() - 1
    me = lax.axis_index(axis)
    y = x[None]
    for j in reversed(range(k)):
        mine = (me >> j) & 1
        got = lax.ppermute(y, axis, [(i, i ^ (1 << j)) for i in range(n)])
        low = jnp.where(mine == 0, y, got)
        high = jnp.where(mine == 0, got, y)
        y = jnp.stack([low, high], 1).reshape((-1,) + x.shape)
    return y.reshape((-1,) + x.shape[1:])


def reduce_then_gather(x, right, axis, n, riders=None):
    k = n.bit_length() - 1
    me = lax.axis_index(axis)
    rows = x.shape[0] // n
    y = x.reshape((2,) * k + (rows,) + x.shape[1:])
    r = right.reshape(y.shape)
    for j in range(k - 1):
        bit_axis = k - 1 - j
        mine = (me >> j) & 1
        keep = lax.dynamic_index_in_dim(y, mine, bit_axis, keepdims=False)
        send = lax.dynamic_index_in_dim(y, 1 - mine, bit_axis, keepdims=False)
        r = lax.dynamic_index_in_dim(r, mine, bit_axis, keepdims=False)
        got = lax.ppermute(send, axis, [(i, i ^ (1 << j)) for i in range(n)])
        if j == 1 and riders is not None:
            got, riders = lax.optimization_barrier((got, riders))
        y = keep + got
    top = k - 1
    y = y + lax.ppermute(y, axis, [(i, i ^ (1 << top)) for i in range(n)])
    y = r - y
    for j in reversed(range(k - 1)):
        mine = (me >> j) & 1
        got = lax.ppermute(y, axis, [(i, i ^ (1 << j)) for i in range(n)])
        low = jnp.where(mine == 0, y, got)
        high = jnp.where(mine == 0, got, y)
        y = jnp.stack([low, high], k - 1 - j)
    return y.reshape(x.shape), riders


def make_shards(n, m):
    power_of_two = n > 1 and (n & (n - 1)) == 0
    rhs_power_of_two = m > 1 and (m & (m - 1)) == 0

    def sum_scatter(x, riders=None):
        if power_of_two and n >= 4:
            return halving_sum_scatter(x, "blk", n, riders)
        return lax.psum_scatter(x, "blk", scatter_dimension=0, tiled=True), riders

    def gather(x):
        if power_of_two:
            return doubling_gather(x, "blk", n)
        return lax.all_gather(x, "blk", axis=0, tiled=True)

    def shards(factor_panel, solved_before, right_side, diag_inverse, coupling):
        if rhs_power_of_two:
            inverse_pieces = doubling_gather(diag_inverse[None], "rhs", m)
        else:
            inverse_pieces = lax.all_gather(diag_inverse, "rhs", axis=0)
        own_count = diag_inverse.shape[1]
        my_index = lax.axis_index("blk")

        def own_slice(matrix):
            return lax.dynamic_slice_in_dim(matrix, my_index * own_count, own_count, 0)

        first_sum = product(factor_panel[0], solved_before)
        first_sum, inverse_pieces = lax.optimization_barrier((first_sum, inverse_pieces))
        inverse_full = jnp.concatenate(list(inverse_pieces), axis=2)
        panel_sum = product(factor_panel[1], solved_before)
        if power_of_two and n >= 4:
            first_remains, panel_sum = reduce_then_gather(first_sum, right_side[0], "blk", n, panel_sum)
        else:
            first_part, panel_sum = sum_scatter(first_sum, panel_sum)
            first_remains = gather(own_slice(right_side[0]) - first_part)
        first_block = product(inverse_full[0], first_remains)
        second_sum = panel_sum + product(coupling, first_block)
        if power_of_two and n >= 4:
            second_remains, _ = reduce_then_gather(second_sum, right_side[1], "blk", n)
        else:
            second_part, _ = sum_scatter(second_sum)
            second_remains = gather(own_slice(right_side[1]) - second_part)
        second_block = product(inverse_full[1], second_remains)
        return jnp.stack([first_block, second_block])

    return shards


def solution(mesh):
    placed = (
        P(None, None, "blk"),
        P("blk", "rhs"),
        P(None, None, "rhs"),
        P(None, "blk", "rhs"),
        P(None, "blk"),
    )
    return jax.shard_map(
        make_shards(mesh.shape["blk"], mesh.shape["rhs"]), mesh=mesh, in_specs=placed, out_specs=P(None, "blk", "rhs"), check_vma=False
    )
```

```python
import jax
import jax.numpy as jnp
from jax import lax
from jax.sharding import PartitionSpec as P


def product(left, right):
    return jnp.dot(left, right, precision=lax.Precision.HIGH, preferred_element_type=jnp.float32)


def halving_sum_scatter(x, axis, n, riders=None):
    k = n.bit_length() - 1
    me = lax.axis_index(axis)
    rows = x.shape[0] // n
    y = x.reshape((2,) * k + (rows,) + x.shape[1:])
    for j in range(k):
        bit_axis = k - 1 - j
        mine = (me >> j) & 1
        keep = lax.dynamic_index_in_dim(y, mine, bit_axis, keepdims=False)
        send = lax.dynamic_index_in_dim(y, 1 - mine, bit_axis, keepdims=False)
        got = lax.ppermute(send, axis, [(i, i ^ (1 << j)) for i in range(n)])
        if j == 1 and riders is not None:
            got, riders = lax.optimization_barrier((got, riders))
        y = keep + got
    return y.reshape((rows,) + x.shape[1:]), riders


def doubling_gather(x, axis, n):
    k = n.bit_length() - 1
    me = lax.axis_index(axis)
    y = x[None]
    for j in reversed(range(k)):
        mine = (me >> j) & 1
        got = lax.ppermute(y, axis, [(i, i ^ (1 << j)) for i in range(n)])
        low = jnp.where(mine == 0, y, got)
        high = jnp.where(mine == 0, got, y)
        y = jnp.stack([low, high], 1).reshape((-1,) + x.shape)
    return y.reshape((-1,) + x.shape[1:])


def reduce_then_gather(x, right, axis, n, riders=None):
    k = n.bit_length() - 1
    me = lax.axis_index(axis)
    rows = x.shape[0] // n
    y = x.reshape((2,) * k + (rows,) + x.shape[1:])
    r = right.reshape(y.shape)
    for j in range(k - 1):
        bit_axis = k - 1 - j
        mine = (me >> j) & 1
        keep = lax.dynamic_index_in_dim(y, mine, bit_axis, keepdims=False)
        send = lax.dynamic_index_in_dim(y, 1 - mine, bit_axis, keepdims=False)
        r = lax.dynamic_index_in_dim(r, mine, bit_axis, keepdims=False)
        got = lax.ppermute(send, axis, [(i, i ^ (1 << j)) for i in range(n)])
        if j == 1 and riders is not None:
            got, riders = lax.optimization_barrier((got, riders))
        y = keep + got
    top = k - 1
    y = y + lax.ppermute(y, axis, [(i, i ^ (1 << top)) for i in range(n)])
    y = r - y
    for j in reversed(range(k - 1)):
        mine = (me >> j) & 1
        got = lax.ppermute(y, axis, [(i, i ^ (1 << j)) for i in range(n)])
        low = jnp.where(mine == 0, y, got)
        high = jnp.where(mine == 0, got, y)
        y = jnp.stack([low, high], k - 1 - j)
    return y.reshape(x.shape), riders


def make_shards(n, m):
    power_of_two = n > 1 and (n & (n - 1)) == 0
    rhs_power_of_two = m > 1 and (m & (m - 1)) == 0

    def sum_scatter(x, riders=None):
        if power_of_two and n >= 4:
            return halving_sum_scatter(x, "blk", n, riders)
        return lax.psum_scatter(x, "blk", scatter_dimension=0, tiled=True), riders

    def gather(x):
        if power_of_two:
            return doubling_gather(x, "blk", n)
        return lax.all_gather(x, "blk", axis=0, tiled=True)

    def shards(factor_panel, solved_before, right_side, diag_inverse, coupling):
        if rhs_power_of_two:
            inverse_pieces = doubling_gather(diag_inverse[None], "rhs", m)
        else:
            inverse_pieces = lax.all_gather(diag_inverse, "rhs", axis=0)
        own_count = diag_inverse.shape[1]
        my_index = lax.axis_index("blk")

        def own_slice(matrix):
            return lax.dynamic_slice_in_dim(matrix, my_index * own_count, own_count, 0)

        first_sum = product(factor_panel[0], solved_before)
        first_sum, inverse_pieces = lax.optimization_barrier((first_sum, inverse_pieces))
        inverse_full = jnp.concatenate(list(inverse_pieces), axis=2)
        panel_sum = product(factor_panel[1], solved_before)
        if power_of_two and n >= 4:
            first_remains, panel_sum = reduce_then_gather(first_sum, right_side[0], "blk", n, panel_sum)
        else:
            first_part, panel_sum = sum_scatter(first_sum, panel_sum)
            first_remains = gather(own_slice(right_side[0]) - first_part)
        first_block = product(inverse_full[0], first_remains)
        second_sum = panel_sum + product(coupling, first_block)
        if power_of_two and n >= 4:
            second_remains, _ = reduce_then_gather(second_sum, right_side[1], "blk", n)
        else:
            second_part, _ = sum_scatter(second_sum)
            second_remains = gather(own_slice(right_side[1]) - second_part)
        second_block = product(inverse_full[1], second_remains)
        return jnp.stack([first_block, second_block])

    return shards


def solution(mesh):
    placed = (
        P(None, None, "blk"),
        P("blk", "rhs"),
        P(None, None, "rhs"),
        P(None, "blk", "rhs"),
        P(None, "blk"),
    )
    return jax.shard_map(
        make_shards(mesh.shape["blk"], mesh.shape["rhs"]), mesh=mesh, in_specs=placed, out_specs=P(None, "blk", "rhs"), check_vma=False
    )
```

```python
import jax
import jax.numpy as jnp
from jax import lax
from jax.sharding import PartitionSpec as P


def product(left, right):
    return jnp.dot(left, right, precision=lax.Precision.HIGHEST, preferred_element_type=jnp.float32)


def halving_sum_scatter(x, axis, n, riders=None):
    k = n.bit_length() - 1
    me = lax.axis_index(axis)
    rows = x.shape[0] // n
    y = x.reshape((2,) * k + (rows,) + x.shape[1:])
    for j in range(k):
        bit_axis = k - 1 - j
        mine = (me >> j) & 1
        keep = lax.dynamic_index_in_dim(y, mine, bit_axis, keepdims=False)
        send = lax.dynamic_index_in_dim(y, 1 - mine, bit_axis, keepdims=False)
        got = lax.ppermute(send, axis, [(i, i ^ (1 << j)) for i in range(n)])
        if j == 1 and riders is not None:
            got, riders = lax.optimization_barrier((got, riders))
        y = keep + got
    return y.reshape((rows,) + x.shape[1:]), riders


def doubling_gather(x, axis, n):
    k = n.bit_length() - 1
    me = lax.axis_index(axis)
    y = x[None]
    for j in reversed(range(k)):
        mine = (me >> j) & 1
        got = lax.ppermute(y, axis, [(i, i ^ (1 << j)) for i in range(n)])
        low = jnp.where(mine == 0, y, got)
        high = jnp.where(mine == 0, got, y)
        y = jnp.stack([low, high], 1).reshape((-1,) + x.shape)
    return y.reshape((-1,) + x.shape[1:])


def reduce_then_gather(x, right, axis, n, riders=None):
    k = n.bit_length() - 1
    me = lax.axis_index(axis)
    rows = x.shape[0] // n
    y = x.reshape((2,) * k + (rows,) + x.shape[1:])
    r = right.reshape(y.shape)
    for j in range(k - 1):
        bit_axis = k - 1 - j
        mine = (me >> j) & 1
        keep = lax.dynamic_index_in_dim(y, mine, bit_axis, keepdims=False)
        send = lax.dynamic_index_in_dim(y, 1 - mine, bit_axis, keepdims=False)
        r = lax.dynamic_index_in_dim(r, mine, bit_axis, keepdims=False)
        got = lax.ppermute(send, axis, [(i, i ^ (1 << j)) for i in range(n)])
        if j == 1 and riders is not None:
            got, riders = lax.optimization_barrier((got, riders))
        y = keep + got
    top = k - 1
    y = y + lax.ppermute(y, axis, [(i, i ^ (1 << top)) for i in range(n)])
    y = r - y
    for j in reversed(range(k - 1)):
        mine = (me >> j) & 1
        got = lax.ppermute(y, axis, [(i, i ^ (1 << j)) for i in range(n)])
        low = jnp.where(mine == 0, y, got)
        high = jnp.where(mine == 0, got, y)
        y = jnp.stack([low, high], k - 1 - j)
    return y.reshape(x.shape), riders


def halves_reduce_then_gather(keep, send, right, axis, n, hold=None, riders_of=None):
    k = n.bit_length() - 1
    me = lax.axis_index(axis)
    half = keep.shape[0]
    mine = me & 1
    r = lax.dynamic_slice_in_dim(right, mine * half, half, 0)
    got = lax.ppermute(send, axis, [(i, i ^ 1) for i in range(n)])
    y = lax.optimization_barrier(keep) + got
    riders = None
    if riders_of is not None:
        y, hold = lax.optimization_barrier((y, hold))
        riders = riders_of(hold)
    for j in range(1, k - 1):
        half //= 2
        mine = (me >> j) & 1
        keep = lax.dynamic_slice_in_dim(y, mine * half, half, 0)
        send = lax.dynamic_slice_in_dim(y, (1 - mine) * half, half, 0)
        r = lax.dynamic_slice_in_dim(r, mine * half, half, 0)
        got = lax.ppermute(send, axis, [(i, i ^ (1 << j)) for i in range(n)])
        if j == 1 and riders is not None:
            got, riders = lax.optimization_barrier((got, riders))
        y = keep + got
    top = k - 1
    y = y + lax.ppermute(y, axis, [(i, i ^ (1 << top)) for i in range(n)])
    y = r - y
    for j in reversed(range(k - 1)):
        mine = (me >> j) & 1
        got = lax.ppermute(y, axis, [(i, i ^ (1 << j)) for i in range(n)])
        low = jnp.where(mine == 0, y, got)
        high = jnp.where(mine == 0, got, y)
        y = jnp.concatenate([low, high], 0)
    return y, riders


def make_shards(n, m):
    power_of_two = n > 1 and (n & (n - 1)) == 0
    rhs_power_of_two = m > 1 and (m & (m - 1)) == 0

    def sum_scatter(x, riders=None):
        if power_of_two and n >= 4:
            return halving_sum_scatter(x, "blk", n, riders)
        return lax.psum_scatter(x, "blk", scatter_dimension=0, tiled=True), riders

    def gather(x):
        if power_of_two:
            return doubling_gather(x, "blk", n)
        return lax.all_gather(x, "blk", axis=0, tiled=True)

    def shards(factor_panel, solved_before, right_side, diag_inverse, coupling):
        if rhs_power_of_two:
            inverse_pieces = doubling_gather(diag_inverse[None], "rhs", m)
        else:
            inverse_pieces = lax.all_gather(diag_inverse, "rhs", axis=0)
        own_count = diag_inverse.shape[1]
        my_index = lax.axis_index("blk")

        def own_slice(matrix):
            return lax.dynamic_slice_in_dim(matrix, my_index * own_count, own_count, 0)

        rows = factor_panel.shape[1]
        split = power_of_two and n >= 4
        if split:
            core = my_index & 1

            def rows_half(matrix, which):
                return lax.dynamic_slice_in_dim(matrix, which * (rows // 2), rows // 2, 0)

            stacked_panel = factor_panel.reshape(2 * rows, -1)
            first_send = product(rows_half(stacked_panel, 1 - core), solved_before)
            first_keep = product(rows_half(stacked_panel, core), solved_before)
        else:
            first_sum = product(factor_panel[0], solved_before)
            first_sum, inverse_pieces = lax.optimization_barrier((first_sum, inverse_pieces))
            panel_sum = product(factor_panel[1], solved_before)
        if split:
            first_remains, (panel_sum, inverse_pieces) = halves_reduce_then_gather(
                first_keep, first_send, right_side[0], "blk", n, (solved_before, inverse_pieces),
                lambda held: (product(factor_panel[1], held[0]), held[1]),
            )
        else:
            first_part, panel_sum = sum_scatter(first_sum, panel_sum)
            first_remains = gather(own_slice(right_side[0]) - first_part)
        inverse_full = jnp.concatenate(list(inverse_pieces), axis=2)
        first_block = product(inverse_full[0], first_remains)
        if split:
            second_send = rows_half(panel_sum, 1 - core) + product(rows_half(coupling, 1 - core), first_block)
            second_keep = rows_half(panel_sum, core) + product(rows_half(coupling, core), first_block)
            second_remains, _ = halves_reduce_then_gather(second_keep, second_send, right_side[1], "blk", n)
        else:
            second_sum = panel_sum + product(coupling, first_block)
            second_part, _ = sum_scatter(second_sum)
            second_remains = gather(own_slice(right_side[1]) - second_part)
        second_block = product(inverse_full[1], second_remains)
        return jnp.stack([first_block, second_block])

    return shards


def solution(mesh):
    placed = (
        P(None, None, "blk"),
        P("blk", "rhs"),
        P(None, None, "rhs"),
        P(None, "blk", "rhs"),
        P(None, "blk"),
    )
    return jax.shard_map(
        make_shards(mesh.shape["blk"], mesh.shape["rhs"]), mesh=mesh, in_specs=placed, out_specs=P(None, "blk", "rhs"), check_vma=False
    )
```

```python
import jax
import jax.numpy as jnp
from jax import lax
from jax.sharding import PartitionSpec as P


def product(left, right):
    return jnp.dot(left, right, precision=lax.Precision.HIGHEST, preferred_element_type=jnp.float32)


def halving_sum_scatter(x, axis, n, riders=None):
    k = n.bit_length() - 1
    me = lax.axis_index(axis)
    rows = x.shape[0] // n
    y = x.reshape((2,) * k + (rows,) + x.shape[1:])
    for j in range(k):
        bit_axis = k - 1 - j
        mine = (me >> j) & 1
        keep = lax.dynamic_index_in_dim(y, mine, bit_axis, keepdims=False)
        send = lax.dynamic_index_in_dim(y, 1 - mine, bit_axis, keepdims=False)
        got = lax.ppermute(send, axis, [(i, i ^ (1 << j)) for i in range(n)])
        if j == 1 and riders is not None:
            got, riders = lax.optimization_barrier((got, riders))
        y = keep + got
    return y.reshape((rows,) + x.shape[1:]), riders


def doubling_gather(x, axis, n):
    k = n.bit_length() - 1
    me = lax.axis_index(axis)
    y = x[None]
    for j in reversed(range(k)):
        mine = (me >> j) & 1
        got = lax.ppermute(y, axis, [(i, i ^ (1 << j)) for i in range(n)])
        low = jnp.where(mine == 0, y, got)
        high = jnp.where(mine == 0, got, y)
        y = jnp.stack([low, high], 1).reshape((-1,) + x.shape)
    return y.reshape((-1,) + x.shape[1:])


def reduce_then_gather(x, right, axis, n, riders=None):
    k = n.bit_length() - 1
    me = lax.axis_index(axis)
    rows = x.shape[0] // n
    y = x.reshape((2,) * k + (rows,) + x.shape[1:])
    r = right.reshape(y.shape)
    for j in range(k - 1):
        bit_axis = k - 1 - j
        mine = (me >> j) & 1
        keep = lax.dynamic_index_in_dim(y, mine, bit_axis, keepdims=False)
        send = lax.dynamic_index_in_dim(y, 1 - mine, bit_axis, keepdims=False)
        r = lax.dynamic_index_in_dim(r, mine, bit_axis, keepdims=False)
        got = lax.ppermute(send, axis, [(i, i ^ (1 << j)) for i in range(n)])
        if j == 1 and riders is not None:
            got, riders = lax.optimization_barrier((got, riders))
        y = keep + got
    top = k - 1
    y = y + lax.ppermute(y, axis, [(i, i ^ (1 << top)) for i in range(n)])
    y = r - y
    for j in reversed(range(k - 1)):
        mine = (me >> j) & 1
        got = lax.ppermute(y, axis, [(i, i ^ (1 << j)) for i in range(n)])
        low = jnp.where(mine == 0, y, got)
        high = jnp.where(mine == 0, got, y)
        y = jnp.stack([low, high], k - 1 - j)
    return y.reshape(x.shape), riders


def reduce_then_apply(x, right, inverse_rows, axis, n, riders=None):
    k = n.bit_length() - 1
    me = lax.axis_index(axis)
    half = x.shape[0]
    y, r = x, right
    for j in range(k - 1):
        half //= 2
        mine = (me >> j) & 1
        keep = lax.dynamic_slice_in_dim(y, mine * half, half, 0)
        send = lax.dynamic_slice_in_dim(y, (1 - mine) * half, half, 0)
        r = lax.dynamic_slice_in_dim(r, mine * half, half, 0)
        got = lax.ppermute(send, axis, [(i, i ^ (1 << j)) for i in range(n)])
        if j == 1 and riders is not None:
            got, riders = lax.optimization_barrier((got, riders))
        y = keep + got
    top = k - 1
    y = y + lax.ppermute(y, axis, [(i, i ^ (1 << top)) for i in range(n)])
    y = r - y
    for j in reversed(range(1, k - 1)):
        mine = (me >> j) & 1
        got = lax.ppermute(y, axis, [(i, i ^ (1 << j)) for i in range(n)])
        low = jnp.where(mine == 0, y, got)
        high = jnp.where(mine == 0, got, y)
        y = jnp.concatenate([low, high], 0)
    mine = me & 1
    got = lax.ppermute(y, axis, [(i, i ^ 1) for i in range(n)])
    half = y.shape[0]
    own_columns = lax.dynamic_slice_in_dim(inverse_rows, mine * half, half, 1)
    other_columns = lax.dynamic_slice_in_dim(inverse_rows, (1 - mine) * half, half, 1)
    return product(own_columns, y) + product(other_columns, got), riders


def make_shards(n, m):
    power_of_two = n > 1 and (n & (n - 1)) == 0
    rhs_power_of_two = m > 1 and (m & (m - 1)) == 0

    def sum_scatter(x, riders=None):
        if power_of_two and n >= 4:
            return halving_sum_scatter(x, "blk", n, riders)
        return lax.psum_scatter(x, "blk", scatter_dimension=0, tiled=True), riders

    def gather(x):
        if power_of_two:
            return doubling_gather(x, "blk", n)
        return lax.all_gather(x, "blk", axis=0, tiled=True)

    def shards(factor_panel, solved_before, right_side, diag_inverse, coupling):
        if rhs_power_of_two:
            inverse_pieces = doubling_gather(diag_inverse[None], "rhs", m)
        else:
            inverse_pieces = lax.all_gather(diag_inverse, "rhs", axis=0)
        own_count = diag_inverse.shape[1]
        my_index = lax.axis_index("blk")

        def own_slice(matrix):
            return lax.dynamic_slice_in_dim(matrix, my_index * own_count, own_count, 0)

        first_sum = product(factor_panel[0], solved_before)
        first_sum, inverse_pieces = lax.optimization_barrier((first_sum, inverse_pieces))
        inverse_full = jnp.concatenate(list(inverse_pieces), axis=2)
        panel_sum = product(factor_panel[1], solved_before)
        if power_of_two and n >= 4:
            first_block, panel_sum = reduce_then_apply(first_sum, right_side[0], inverse_full[0], "blk", n, panel_sum)
        else:
            first_part, panel_sum = sum_scatter(first_sum, panel_sum)
            first_remains = gather(own_slice(right_side[0]) - first_part)
            first_block = product(inverse_full[0], first_remains)
        second_sum = panel_sum + product(coupling, first_block)
        if power_of_two and n >= 4:
            second_block, _ = reduce_then_apply(second_sum, right_side[1], inverse_full[1], "blk", n)
        else:
            second_part, _ = sum_scatter(second_sum)
            second_remains = gather(own_slice(right_side[1]) - second_part)
            second_block = product(inverse_full[1], second_remains)
        return jnp.stack([first_block, second_block])

    return shards


def solution(mesh):
    placed = (
        P(None, None, "blk"),
        P("blk", "rhs"),
        P(None, None, "rhs"),
        P(None, "blk", "rhs"),
        P(None, "blk"),
    )
    return jax.shard_map(
        make_shards(mesh.shape["blk"], mesh.shape["rhs"]), mesh=mesh, in_specs=placed, out_specs=P(None, "blk", "rhs"), check_vma=False
    )
```

```python
import jax
import jax.numpy as jnp
from jax import lax
from jax.sharding import PartitionSpec as P


def product(left, right):
    return jnp.dot(left, right, precision=lax.Precision.HIGHEST, preferred_element_type=jnp.float32)


def halving_sum_scatter(x, axis, n, riders=None):
    k = n.bit_length() - 1
    me = lax.axis_index(axis)
    rows = x.shape[0] // n
    y = x.reshape((2,) * k + (rows,) + x.shape[1:])
    for j in range(k):
        bit_axis = k - 1 - j
        mine = (me >> j) & 1
        keep = lax.dynamic_index_in_dim(y, mine, bit_axis, keepdims=False)
        send = lax.dynamic_index_in_dim(y, 1 - mine, bit_axis, keepdims=False)
        got = lax.ppermute(send, axis, [(i, i ^ (1 << j)) for i in range(n)])
        if j == 1 and riders is not None:
            got, riders = lax.optimization_barrier((got, riders))
        y = keep + got
    return y.reshape((rows,) + x.shape[1:]), riders


def doubling_gather(x, axis, n):
    k = n.bit_length() - 1
    me = lax.axis_index(axis)
    y = x[None]
    for j in reversed(range(k)):
        mine = (me >> j) & 1
        got = lax.ppermute(y, axis, [(i, i ^ (1 << j)) for i in range(n)])
        low = jnp.where(mine == 0, y, got)
        high = jnp.where(mine == 0, got, y)
        y = jnp.stack([low, high], 1).reshape((-1,) + x.shape)
    return y.reshape((-1,) + x.shape[1:])


def reduce_then_gather(x, right, axis, n, riders=None):
    k = n.bit_length() - 1
    me = lax.axis_index(axis)
    rows = x.shape[0] // n
    y = x.reshape((2,) * k + (rows,) + x.shape[1:])
    r = right.reshape(y.shape)
    for j in range(k - 1):
        bit_axis = k - 1 - j
        mine = (me >> j) & 1
        keep = lax.dynamic_index_in_dim(y, mine, bit_axis, keepdims=False)
        send = lax.dynamic_index_in_dim(y, 1 - mine, bit_axis, keepdims=False)
        r = lax.dynamic_index_in_dim(r, mine, bit_axis, keepdims=False)
        got = lax.ppermute(send, axis, [(i, i ^ (1 << j)) for i in range(n)])
        if j == 1 and riders is not None:
            got, riders = lax.optimization_barrier((got, riders))
        y = keep + got
    top = k - 1
    y = y + lax.ppermute(y, axis, [(i, i ^ (1 << top)) for i in range(n)])
    y = r - y
    for j in reversed(range(k - 1)):
        mine = (me >> j) & 1
        got = lax.ppermute(y, axis, [(i, i ^ (1 << j)) for i in range(n)])
        low = jnp.where(mine == 0, y, got)
        high = jnp.where(mine == 0, got, y)
        y = jnp.stack([low, high], k - 1 - j)
    return y.reshape(x.shape), riders


def ordered_reduce_then_gather(x, right, axis, n, order, riders=None):
    me = lax.axis_index(axis)
    y, r = x, right
    for step, j in enumerate(order[:-1]):
        half = y.shape[0] // 2
        mine = (me >> j) & 1
        keep = lax.dynamic_slice_in_dim(y, mine * half, half, 0)
        send = lax.dynamic_slice_in_dim(y, (1 - mine) * half, half, 0)
        r = lax.dynamic_slice_in_dim(r, mine * half, half, 0)
        got = lax.ppermute(send, axis, [(i, i ^ (1 << j)) for i in range(n)])
        if step == 1 and riders is not None:
            got, riders = lax.optimization_barrier((got, riders))
        y = keep + got
    top = order[-1]
    y = y + lax.ppermute(y, axis, [(i, i ^ (1 << top)) for i in range(n)])
    y = r - y
    for j in reversed(order[:-1]):
        mine = (me >> j) & 1
        got = lax.ppermute(y, axis, [(i, i ^ (1 << j)) for i in range(n)])
        low = jnp.where(mine == 0, y, got)
        high = jnp.where(mine == 0, got, y)
        y = jnp.concatenate([low, high], 0)
    return y, riders


def make_shards(n, m):
    power_of_two = n > 1 and (n & (n - 1)) == 0
    rhs_power_of_two = m > 1 and (m & (m - 1)) == 0

    def sum_scatter(x, riders=None):
        if power_of_two and n >= 4:
            return halving_sum_scatter(x, "blk", n, riders)
        return lax.psum_scatter(x, "blk", scatter_dimension=0, tiled=True), riders

    def gather(x):
        if power_of_two:
            return doubling_gather(x, "blk", n)
        return lax.all_gather(x, "blk", axis=0, tiled=True)

    def shards(factor_panel, solved_before, right_side, diag_inverse, coupling):
        if rhs_power_of_two:
            inverse_pieces = doubling_gather(diag_inverse[None], "rhs", m)
        else:
            inverse_pieces = lax.all_gather(diag_inverse, "rhs", axis=0)
        own_count = diag_inverse.shape[1]
        my_index = lax.axis_index("blk")

        def own_slice(matrix):
            return lax.dynamic_slice_in_dim(matrix, my_index * own_count, own_count, 0)

        first_sum = product(factor_panel[0], solved_before)
        first_sum, inverse_pieces = lax.optimization_barrier((first_sum, inverse_pieces))
        inverse_full = jnp.concatenate(list(inverse_pieces), axis=2)
        panel_sum = product(factor_panel[1], solved_before)
        if power_of_two and n >= 4:
            k = n.bit_length() - 1
            orders = (list(range(k)), [0, 2, 1] + list(range(3, k)) if k >= 3 else list(range(k)))
            width = first_sum.shape[1] // 2
            columns = (slice(0, width), slice(width, 2 * width))
            first_blocks = []
            for chain, (order, cols) in enumerate(zip(orders, columns)):
                remains, got_riders = ordered_reduce_then_gather(
                    first_sum[:, cols], right_side[0][:, cols], "blk", n, order,
                    (panel_sum, inverse_pieces) if chain == 0 else None,
                )
                if chain == 0:
                    panel_sum, inverse_pieces = got_riders
                first_blocks.append(remains)
            inverse_full = jnp.concatenate(list(inverse_pieces), axis=2)
            first_blocks = [product(inverse_full[0], remains) for remains in first_blocks]
            second_blocks = []
            for order, cols, block in zip(orders, columns, first_blocks):
                remains, _ = ordered_reduce_then_gather(
                    panel_sum[:, cols] + product(coupling, block), right_side[1][:, cols], "blk", n, order
                )
                second_blocks.append(product(inverse_full[1], remains))
            first_block = jnp.concatenate(first_blocks, 1)
            second_block = jnp.concatenate(second_blocks, 1)
        else:
            inverse_full = jnp.concatenate(list(inverse_pieces), axis=2)
            first_part, panel_sum = sum_scatter(first_sum, panel_sum)
            first_remains = gather(own_slice(right_side[0]) - first_part)
            first_block = product(inverse_full[0], first_remains)
            second_part, _ = sum_scatter(panel_sum + product(coupling, first_block))
            second_remains = gather(own_slice(right_side[1]) - second_part)
            second_block = product(inverse_full[1], second_remains)
        return jnp.stack([first_block, second_block])

    return shards


def solution(mesh):
    placed = (
        P(None, None, "blk"),
        P("blk", "rhs"),
        P(None, None, "rhs"),
        P(None, "blk", "rhs"),
        P(None, "blk"),
    )
    return jax.shard_map(
        make_shards(mesh.shape["blk"], mesh.shape["rhs"]), mesh=mesh, in_specs=placed, out_specs=P(None, "blk", "rhs"), check_vma=False
    )
```

```python
import jax
import jax.numpy as jnp
from jax import lax
from jax.sharding import PartitionSpec as P


def product(left, right):
    return jnp.dot(left, right, precision=lax.Precision.HIGHEST, preferred_element_type=jnp.float32)


def halving_sum_scatter(x, axis, n, riders=None):
    k = n.bit_length() - 1
    me = lax.axis_index(axis)
    rows = x.shape[0] // n
    y = x.reshape((2,) * k + (rows,) + x.shape[1:])
    for j in range(k):
        bit_axis = k - 1 - j
        mine = (me >> j) & 1
        keep = lax.dynamic_index_in_dim(y, mine, bit_axis, keepdims=False)
        send = lax.dynamic_index_in_dim(y, 1 - mine, bit_axis, keepdims=False)
        got = lax.ppermute(send, axis, [(i, i ^ (1 << j)) for i in range(n)])
        if j == 1 and riders is not None:
            got, riders = lax.optimization_barrier((got, riders))
        y = keep + got
    return y.reshape((rows,) + x.shape[1:]), riders


def doubling_gather(x, axis, n):
    k = n.bit_length() - 1
    me = lax.axis_index(axis)
    y = x[None]
    for j in reversed(range(k)):
        mine = (me >> j) & 1
        got = lax.ppermute(y, axis, [(i, i ^ (1 << j)) for i in range(n)])
        low = jnp.where(mine == 0, y, got)
        high = jnp.where(mine == 0, got, y)
        y = jnp.stack([low, high], 1).reshape((-1,) + x.shape)
    return y.reshape((-1,) + x.shape[1:])


def reduce_then_gather(x, right, axis, n, riders=None):
    k = n.bit_length() - 1
    me = lax.axis_index(axis)
    rows = x.shape[0] // n
    y = x.reshape((2,) * k + (rows,) + x.shape[1:])
    r = right.reshape(y.shape)
    for j in range(k - 1):
        bit_axis = k - 1 - j
        mine = (me >> j) & 1
        keep = lax.dynamic_index_in_dim(y, mine, bit_axis, keepdims=False)
        send = lax.dynamic_index_in_dim(y, 1 - mine, bit_axis, keepdims=False)
        r = lax.dynamic_index_in_dim(r, mine, bit_axis, keepdims=False)
        got = lax.ppermute(send, axis, [(i, i ^ (1 << j)) for i in range(n)])
        if j == 1 and riders is not None:
            got, riders = lax.optimization_barrier((got, riders))
        y = keep + got
    top = k - 1
    y = y + lax.ppermute(y, axis, [(i, i ^ (1 << top)) for i in range(n)])
    y = r - y
    for j in reversed(range(k - 1)):
        mine = (me >> j) & 1
        got = lax.ppermute(y, axis, [(i, i ^ (1 << j)) for i in range(n)])
        low = jnp.where(mine == 0, y, got)
        high = jnp.where(mine == 0, got, y)
        y = jnp.stack([low, high], k - 1 - j)
    return y.reshape(x.shape), riders


def ordered_reduce_then_gather(x, right, axis, n, order, riders=None):
    me = lax.axis_index(axis)
    y, r = x, right
    for step, j in enumerate(order[:-1]):
        half = y.shape[0] // 2
        mine = (me >> j) & 1
        keep = lax.dynamic_slice_in_dim(y, mine * half, half, 0)
        send = lax.dynamic_slice_in_dim(y, (1 - mine) * half, half, 0)
        r = lax.dynamic_slice_in_dim(r, mine * half, half, 0)
        got = lax.ppermute(send, axis, [(i, i ^ (1 << j)) for i in range(n)])
        if step == 1 and riders is not None:
            got, riders = lax.optimization_barrier((got, riders))
        y = keep + got
    top = order[-1]
    y = y + lax.ppermute(y, axis, [(i, i ^ (1 << top)) for i in range(n)])
    y = r - y
    for j in reversed(order[:-1]):
        mine = (me >> j) & 1
        got = lax.ppermute(y, axis, [(i, i ^ (1 << j)) for i in range(n)])
        low = jnp.where(mine == 0, y, got)
        high = jnp.where(mine == 0, got, y)
        y = jnp.concatenate([low, high], 0)
    return y, riders


def make_shards(n, m):
    power_of_two = n > 1 and (n & (n - 1)) == 0
    rhs_power_of_two = m > 1 and (m & (m - 1)) == 0

    def sum_scatter(x, riders=None):
        if power_of_two and n >= 4:
            return halving_sum_scatter(x, "blk", n, riders)
        return lax.psum_scatter(x, "blk", scatter_dimension=0, tiled=True), riders

    def gather(x):
        if power_of_two:
            return doubling_gather(x, "blk", n)
        return lax.all_gather(x, "blk", axis=0, tiled=True)

    def shards(factor_panel, solved_before, right_side, diag_inverse, coupling):
        if rhs_power_of_two:
            inverse_pieces = doubling_gather(diag_inverse[None], "rhs", m)
        else:
            inverse_pieces = lax.all_gather(diag_inverse, "rhs", axis=0)
        own_count = diag_inverse.shape[1]
        my_index = lax.axis_index("blk")

        def own_slice(matrix):
            return lax.dynamic_slice_in_dim(matrix, my_index * own_count, own_count, 0)

        first_sum = product(factor_panel[0], solved_before)
        first_sum, inverse_pieces = lax.optimization_barrier((first_sum, inverse_pieces))
        inverse_full = jnp.concatenate(list(inverse_pieces), axis=2)
        panel_sum = product(factor_panel[1], solved_before)
        if power_of_two and n >= 4:
            k = n.bit_length() - 1
            orders = (list(range(k)), [0, 2, 1] + list(range(3, k)) if k >= 3 else list(range(k)))
            width = first_sum.shape[1] // 2
            height = first_sum.shape[0] // 2
            columns = (slice(0, width), slice(width, 2 * width))
            row_parts = (slice(0, height), slice(height, 2 * height))
            pieces = [(rows, cols, orders[(a + b) % 2]) for a, rows in enumerate(row_parts) for b, cols in enumerate(columns)]
            first_remains = []
            for chain, (rows, cols, order) in enumerate(pieces):
                remains, got_riders = ordered_reduce_then_gather(
                    first_sum[rows, cols], right_side[0][rows, cols], "blk", n, order,
                    (panel_sum, inverse_pieces) if chain == 0 else None,
                )
                if chain == 0:
                    panel_sum, inverse_pieces = got_riders
                first_remains.append(remains)
            inverse_full = jnp.concatenate(list(inverse_pieces), axis=2)

            def apply(matrix, parts):
                return [
                    sum(product(matrix[:, rows], parts[a * 2 + b]) for a, rows in enumerate(row_parts))
                    for b in range(2)
                ]

            first_blocks = apply(inverse_full[0], first_remains)
            second_remains = []
            for rows, cols, order in pieces:
                b = 0 if cols.start == 0 else 1
                remains, _ = ordered_reduce_then_gather(
                    panel_sum[rows, cols] + product(coupling[rows], first_blocks[b]), right_side[1][rows, cols], "blk", n, order
                )
                second_remains.append(remains)
            second_blocks = apply(inverse_full[1], second_remains)
            first_block = jnp.concatenate(first_blocks, 1)
            second_block = jnp.concatenate(second_blocks, 1)
        else:
            inverse_full = jnp.concatenate(list(inverse_pieces), axis=2)
            first_part, panel_sum = sum_scatter(first_sum, panel_sum)
            first_remains = gather(own_slice(right_side[0]) - first_part)
            first_block = product(inverse_full[0], first_remains)
            second_part, _ = sum_scatter(panel_sum + product(coupling, first_block))
            second_remains = gather(own_slice(right_side[1]) - second_part)
            second_block = product(inverse_full[1], second_remains)
        return jnp.stack([first_block, second_block])

    return shards


def solution(mesh):
    placed = (
        P(None, None, "blk"),
        P("blk", "rhs"),
        P(None, None, "rhs"),
        P(None, "blk", "rhs"),
        P(None, "blk"),
    )
    return jax.shard_map(
        make_shards(mesh.shape["blk"], mesh.shape["rhs"]), mesh=mesh, in_specs=placed, out_specs=P(None, "blk", "rhs"), check_vma=False
    )
```

```python
import jax
import jax.numpy as jnp
from jax import lax
from jax.sharding import PartitionSpec as P


def product(left, right):
    return jnp.dot(left, right, precision=lax.Precision.HIGHEST, preferred_element_type=jnp.float32)


def halving_sum_scatter(x, axis, n, riders=None):
    k = n.bit_length() - 1
    me = lax.axis_index(axis)
    rows = x.shape[0] // n
    y = x.reshape((2,) * k + (rows,) + x.shape[1:])
    for j in range(k):
        bit_axis = k - 1 - j
        mine = (me >> j) & 1
        keep = lax.dynamic_index_in_dim(y, mine, bit_axis, keepdims=False)
        send = lax.dynamic_index_in_dim(y, 1 - mine, bit_axis, keepdims=False)
        got = lax.ppermute(send, axis, [(i, i ^ (1 << j)) for i in range(n)])
        if j == 1 and riders is not None:
            got, riders = lax.optimization_barrier((got, riders))
        y = keep + got
    return y.reshape((rows,) + x.shape[1:]), riders


def doubling_gather(x, axis, n):
    k = n.bit_length() - 1
    me = lax.axis_index(axis)
    y = x[None]
    for j in reversed(range(k)):
        mine = (me >> j) & 1
        got = lax.ppermute(y, axis, [(i, i ^ (1 << j)) for i in range(n)])
        low = jnp.where(mine == 0, y, got)
        high = jnp.where(mine == 0, got, y)
        y = jnp.stack([low, high], 1).reshape((-1,) + x.shape)
    return y.reshape((-1,) + x.shape[1:])


def reduce_then_gather(x, right, axis, n, riders=None):
    k = n.bit_length() - 1
    me = lax.axis_index(axis)
    rows = x.shape[0] // n
    y = x.reshape((2,) * k + (rows,) + x.shape[1:])
    r = right.reshape(y.shape)
    for j in range(k - 1):
        bit_axis = k - 1 - j
        mine = (me >> j) & 1
        keep = lax.dynamic_index_in_dim(y, mine, bit_axis, keepdims=False)
        send = lax.dynamic_index_in_dim(y, 1 - mine, bit_axis, keepdims=False)
        r = lax.dynamic_index_in_dim(r, mine, bit_axis, keepdims=False)
        got = lax.ppermute(send, axis, [(i, i ^ (1 << j)) for i in range(n)])
        if j == 1 and riders is not None:
            got, riders = lax.optimization_barrier((got, riders))
        y = keep + got
    top = k - 1
    y = y + lax.ppermute(y, axis, [(i, i ^ (1 << top)) for i in range(n)])
    y = r - y
    for j in reversed(range(k - 1)):
        mine = (me >> j) & 1
        got = lax.ppermute(y, axis, [(i, i ^ (1 << j)) for i in range(n)])
        low = jnp.where(mine == 0, y, got)
        high = jnp.where(mine == 0, got, y)
        y = jnp.stack([low, high], k - 1 - j)
    return y.reshape(x.shape), riders


def ordered_reduce_then_gather(x, right, axis, n, order, riders=None, hold=None):
    me = lax.axis_index(axis)
    y, r = x, right
    for step, j in enumerate(order[:-1]):
        half = y.shape[0] // 2
        mine = (me >> j) & 1
        keep = lax.dynamic_slice_in_dim(y, mine * half, half, 0)
        send = lax.dynamic_slice_in_dim(y, (1 - mine) * half, half, 0)
        r = lax.dynamic_slice_in_dim(r, mine * half, half, 0)
        got = lax.ppermute(send, axis, [(i, i ^ (1 << j)) for i in range(n)])
        if step == 1 and riders is not None:
            got, riders = lax.optimization_barrier((got, riders))
        y = keep + got
        if step == 0 and hold is not None:
            y, held = lax.optimization_barrier((y, hold[0]))
            riders = (hold[1](held), riders)
    top = order[-1]
    y = y + lax.ppermute(y, axis, [(i, i ^ (1 << top)) for i in range(n)])
    y = r - y
    for j in reversed(order[:-1]):
        mine = (me >> j) & 1
        got = lax.ppermute(y, axis, [(i, i ^ (1 << j)) for i in range(n)])
        low = jnp.where(mine == 0, y, got)
        high = jnp.where(mine == 0, got, y)
        y = jnp.concatenate([low, high], 0)
    return y, riders


def make_shards(n, m):
    power_of_two = n > 1 and (n & (n - 1)) == 0
    rhs_power_of_two = m > 1 and (m & (m - 1)) == 0

    def sum_scatter(x, riders=None):
        if power_of_two and n >= 4:
            return halving_sum_scatter(x, "blk", n, riders)
        return lax.psum_scatter(x, "blk", scatter_dimension=0, tiled=True), riders

    def gather(x):
        if power_of_two:
            return doubling_gather(x, "blk", n)
        return lax.all_gather(x, "blk", axis=0, tiled=True)

    def shards(factor_panel, solved_before, right_side, diag_inverse, coupling):
        if rhs_power_of_two:
            inverse_pieces = doubling_gather(diag_inverse[None], "rhs", m)
        else:
            inverse_pieces = lax.all_gather(diag_inverse, "rhs", axis=0)
        own_count = diag_inverse.shape[1]
        my_index = lax.axis_index("blk")

        def own_slice(matrix):
            return lax.dynamic_slice_in_dim(matrix, my_index * own_count, own_count, 0)

        chained = power_of_two and n >= 4
        if chained:
            width = solved_before.shape[1] // 2
            column_major = solved_before.reshape(solved_before.shape[0], 2, width)

            def split_product(left, right):
                return jnp.einsum(
                    "ij,jbk->bik", left, right, precision=lax.Precision.HIGHEST, preferred_element_type=jnp.float32
                )

            first_sum = split_product(factor_panel[0], column_major)
            first_sum, inverse_pieces = lax.optimization_barrier((first_sum, inverse_pieces))
        else:
            first_sum = product(factor_panel[0], solved_before)
            first_sum, inverse_pieces = lax.optimization_barrier((first_sum, inverse_pieces))
            panel_sum = product(factor_panel[1], solved_before)
        if chained:
            k = n.bit_length() - 1
            orders = (list(range(k)), [0, 2, 1] + list(range(3, k)) if k >= 3 else list(range(k)))
            columns = (slice(0, width), slice(width, 2 * width))
            first_blocks = []
            for chain, (order, cols) in enumerate(zip(orders, columns)):
                remains, got_riders = ordered_reduce_then_gather(
                    first_sum[chain], right_side[0][:, cols], "blk", n, order,
                    inverse_pieces if chain == 0 else None,
                    (column_major, lambda held: split_product(factor_panel[1], held)) if chain == 0 else None,
                )
                if chain == 0:
                    panel_sum, inverse_pieces = got_riders
                first_blocks.append(remains)
            inverse_full = jnp.concatenate(list(inverse_pieces), axis=2)
            first_blocks = [product(inverse_full[0], remains) for remains in first_blocks]
            second_blocks = []
            for chain, (order, cols, block) in enumerate(zip(orders, columns, first_blocks)):
                remains, _ = ordered_reduce_then_gather(
                    panel_sum[chain] + product(coupling, block), right_side[1][:, cols], "blk", n, order
                )
                second_blocks.append(product(inverse_full[1], remains))
            first_block = jnp.concatenate(first_blocks, 1)
            second_block = jnp.concatenate(second_blocks, 1)
        else:
            inverse_full = jnp.concatenate(list(inverse_pieces), axis=2)
            first_part, panel_sum = sum_scatter(first_sum, panel_sum)
            first_remains = gather(own_slice(right_side[0]) - first_part)
            first_block = product(inverse_full[0], first_remains)
            second_part, _ = sum_scatter(panel_sum + product(coupling, first_block))
            second_remains = gather(own_slice(right_side[1]) - second_part)
            second_block = product(inverse_full[1], second_remains)
        return jnp.stack([first_block, second_block])

    return shards


def solution(mesh):
    placed = (
        P(None, None, "blk"),
        P("blk", "rhs"),
        P(None, None, "rhs"),
        P(None, "blk", "rhs"),
        P(None, "blk"),
    )
    return jax.shard_map(
        make_shards(mesh.shape["blk"], mesh.shape["rhs"]), mesh=mesh, in_specs=placed, out_specs=P(None, "blk", "rhs"), check_vma=False
    )
```

```python
import jax
import jax.numpy as jnp
from jax import lax
from jax.sharding import PartitionSpec as P


def product(left, right):
    return jnp.dot(left, right, precision=lax.Precision.HIGHEST, preferred_element_type=jnp.float32)


def halving_sum_scatter(x, axis, n, riders=None):
    k = n.bit_length() - 1
    me = lax.axis_index(axis)
    rows = x.shape[0] // n
    y = x.reshape((2,) * k + (rows,) + x.shape[1:])
    for j in range(k):
        bit_axis = k - 1 - j
        mine = (me >> j) & 1
        keep = lax.dynamic_index_in_dim(y, mine, bit_axis, keepdims=False)
        send = lax.dynamic_index_in_dim(y, 1 - mine, bit_axis, keepdims=False)
        got = lax.ppermute(send, axis, [(i, i ^ (1 << j)) for i in range(n)])
        if j == 1 and riders is not None:
            got, riders = lax.optimization_barrier((got, riders))
        y = keep + got
    return y.reshape((rows,) + x.shape[1:]), riders


def doubling_gather(x, axis, n):
    k = n.bit_length() - 1
    me = lax.axis_index(axis)
    y = x[None]
    for j in reversed(range(k)):
        mine = (me >> j) & 1
        got = lax.ppermute(y, axis, [(i, i ^ (1 << j)) for i in range(n)])
        low = jnp.where(mine == 0, y, got)
        high = jnp.where(mine == 0, got, y)
        y = jnp.stack([low, high], 1).reshape((-1,) + x.shape)
    return y.reshape((-1,) + x.shape[1:])


def reduce_then_gather(x, right, axis, n, riders=None):
    k = n.bit_length() - 1
    me = lax.axis_index(axis)
    rows = x.shape[0] // n
    y = x.reshape((2,) * k + (rows,) + x.shape[1:])
    r = right.reshape(y.shape)
    for j in range(k - 1):
        bit_axis = k - 1 - j
        mine = (me >> j) & 1
        keep = lax.dynamic_index_in_dim(y, mine, bit_axis, keepdims=False)
        send = lax.dynamic_index_in_dim(y, 1 - mine, bit_axis, keepdims=False)
        r = lax.dynamic_index_in_dim(r, mine, bit_axis, keepdims=False)
        got = lax.ppermute(send, axis, [(i, i ^ (1 << j)) for i in range(n)])
        if j == 1 and riders is not None:
            got, riders = lax.optimization_barrier((got, riders))
        y = keep + got
    top = k - 1
    y = y + lax.ppermute(y, axis, [(i, i ^ (1 << top)) for i in range(n)])
    y = r - y
    for j in reversed(range(k - 1)):
        mine = (me >> j) & 1
        got = lax.ppermute(y, axis, [(i, i ^ (1 << j)) for i in range(n)])
        low = jnp.where(mine == 0, y, got)
        high = jnp.where(mine == 0, got, y)
        y = jnp.stack([low, high], k - 1 - j)
    return y.reshape(x.shape), riders


def ordered_reduce_then_gather(x, right, axis, n, order, riders=None, hold=None):
    me = lax.axis_index(axis)
    y, r = x, right
    for step, j in enumerate(order[:-1]):
        half = y.shape[0] // 2
        mine = (me >> j) & 1
        keep = lax.dynamic_slice_in_dim(y, mine * half, half, 0)
        send = lax.dynamic_slice_in_dim(y, (1 - mine) * half, half, 0)
        r = lax.dynamic_slice_in_dim(r, mine * half, half, 0)
        got = lax.ppermute(send, axis, [(i, i ^ (1 << j)) for i in range(n)])
        if step == 1 and riders is not None:
            got, riders = lax.optimization_barrier((got, riders))
        y = keep + got
        if step == 0 and hold is not None:
            y, held = lax.optimization_barrier((y, hold[0]))
            riders = (hold[1](held), riders)
    top = order[-1]
    y = y + lax.ppermute(y, axis, [(i, i ^ (1 << top)) for i in range(n)])
    y = r - y
    for j in reversed(order[:-1]):
        mine = (me >> j) & 1
        got = lax.ppermute(y, axis, [(i, i ^ (1 << j)) for i in range(n)])
        low = jnp.where(mine == 0, y, got)
        high = jnp.where(mine == 0, got, y)
        y = jnp.concatenate([low, high], 0)
    return y, riders


def make_shards(n, m):
    power_of_two = n > 1 and (n & (n - 1)) == 0
    rhs_power_of_two = m > 1 and (m & (m - 1)) == 0

    def sum_scatter(x, riders=None):
        if power_of_two and n >= 4:
            return halving_sum_scatter(x, "blk", n, riders)
        return lax.psum_scatter(x, "blk", scatter_dimension=0, tiled=True), riders

    def gather(x):
        if power_of_two:
            return doubling_gather(x, "blk", n)
        return lax.all_gather(x, "blk", axis=0, tiled=True)

    def shards(factor_panel, solved_before, right_side, diag_inverse, coupling):
        if rhs_power_of_two:
            inverse_pieces = doubling_gather(diag_inverse[None], "rhs", m)
        else:
            inverse_pieces = lax.all_gather(diag_inverse, "rhs", axis=0)
        own_count = diag_inverse.shape[1]
        my_index = lax.axis_index("blk")

        def own_slice(matrix):
            return lax.dynamic_slice_in_dim(matrix, my_index * own_count, own_count, 0)

        first_sum = product(factor_panel[0], solved_before)
        first_sum, inverse_pieces = lax.optimization_barrier((first_sum, inverse_pieces))
        chained = power_of_two and n >= 4
        if not chained:
            panel_sum = product(factor_panel[1], solved_before)
        if chained:
            k = n.bit_length() - 1
            orders = (list(range(k)), [0, 2, 1] + list(range(3, k)) if k >= 3 else list(range(k)))
            width = first_sum.shape[1] // 2
            columns = (slice(0, width), slice(width, 2 * width))
            first_blocks = []
            for chain, (order, cols) in enumerate(zip(orders, columns)):
                remains, got_riders = ordered_reduce_then_gather(
                    first_sum[:, cols], right_side[0][:, cols], "blk", n, order,
                    inverse_pieces if chain == 0 else None,
                    (solved_before, lambda held: product(factor_panel[1], held)) if chain == 0 else None,
                )
                if chain == 0:
                    panel_sum, inverse_pieces = got_riders
                first_blocks.append(remains)
            inverse_full = jnp.concatenate(list(inverse_pieces), axis=2)
            first_blocks = [product(inverse_full[0], remains) for remains in first_blocks]
            second_blocks = []
            for order, cols, block in zip(orders, columns, first_blocks):
                remains, _ = ordered_reduce_then_gather(
                    panel_sum[:, cols] + product(coupling, block), right_side[1][:, cols], "blk", n, order
                )
                second_blocks.append(product(inverse_full[1], remains))
            first_block = jnp.concatenate(first_blocks, 1)
            second_block = jnp.concatenate(second_blocks, 1)
        else:
            inverse_full = jnp.concatenate(list(inverse_pieces), axis=2)
            first_part, panel_sum = sum_scatter(first_sum, panel_sum)
            first_remains = gather(own_slice(right_side[0]) - first_part)
            first_block = product(inverse_full[0], first_remains)
            second_part, _ = sum_scatter(panel_sum + product(coupling, first_block))
            second_remains = gather(own_slice(right_side[1]) - second_part)
            second_block = product(inverse_full[1], second_remains)
        return jnp.stack([first_block, second_block])

    return shards


def solution(mesh):
    placed = (
        P(None, None, "blk"),
        P("blk", "rhs"),
        P(None, None, "rhs"),
        P(None, "blk", "rhs"),
        P(None, "blk"),
    )
    return jax.shard_map(
        make_shards(mesh.shape["blk"], mesh.shape["rhs"]), mesh=mesh, in_specs=placed, out_specs=P(None, "blk", "rhs"), check_vma=False
    )
```

```python
import jax
import jax.numpy as jnp
from jax import lax
from jax.sharding import PartitionSpec as P


def product(left, right):
    return jnp.dot(left, right, precision=lax.Precision.HIGHEST, preferred_element_type=jnp.float32)


def halving_sum_scatter(x, axis, n, riders=None):
    k = n.bit_length() - 1
    me = lax.axis_index(axis)
    rows = x.shape[0] // n
    y = x.reshape((2,) * k + (rows,) + x.shape[1:])
    for j in range(k):
        bit_axis = k - 1 - j
        mine = (me >> j) & 1
        keep = lax.dynamic_index_in_dim(y, mine, bit_axis, keepdims=False)
        send = lax.dynamic_index_in_dim(y, 1 - mine, bit_axis, keepdims=False)
        got = lax.ppermute(send, axis, [(i, i ^ (1 << j)) for i in range(n)])
        if j == 1 and riders is not None:
            got, riders = lax.optimization_barrier((got, riders))
        y = keep + got
    return y.reshape((rows,) + x.shape[1:]), riders


def doubling_gather(x, axis, n):
    k = n.bit_length() - 1
    me = lax.axis_index(axis)
    y = x[None]
    for j in reversed(range(k)):
        mine = (me >> j) & 1
        got = lax.ppermute(y, axis, [(i, i ^ (1 << j)) for i in range(n)])
        low = jnp.where(mine == 0, y, got)
        high = jnp.where(mine == 0, got, y)
        y = jnp.stack([low, high], 1).reshape((-1,) + x.shape)
    return y.reshape((-1,) + x.shape[1:])


def reduce_then_gather(x, right, axis, n, riders=None):
    k = n.bit_length() - 1
    me = lax.axis_index(axis)
    rows = x.shape[0] // n
    y = x.reshape((2,) * k + (rows,) + x.shape[1:])
    r = right.reshape(y.shape)
    for j in range(k - 1):
        bit_axis = k - 1 - j
        mine = (me >> j) & 1
        keep = lax.dynamic_index_in_dim(y, mine, bit_axis, keepdims=False)
        send = lax.dynamic_index_in_dim(y, 1 - mine, bit_axis, keepdims=False)
        r = lax.dynamic_index_in_dim(r, mine, bit_axis, keepdims=False)
        got = lax.ppermute(send, axis, [(i, i ^ (1 << j)) for i in range(n)])
        if j == 1 and riders is not None:
            got, riders = lax.optimization_barrier((got, riders))
        y = keep + got
    top = k - 1
    y = y + lax.ppermute(y, axis, [(i, i ^ (1 << top)) for i in range(n)])
    y = r - y
    for j in reversed(range(k - 1)):
        mine = (me >> j) & 1
        got = lax.ppermute(y, axis, [(i, i ^ (1 << j)) for i in range(n)])
        low = jnp.where(mine == 0, y, got)
        high = jnp.where(mine == 0, got, y)
        y = jnp.stack([low, high], k - 1 - j)
    return y.reshape(x.shape), riders


def ordered_reduce_then_gather(x, right, axis, n, order, riders=None, hold=None, width=None, column=0):
    me = lax.axis_index(axis)
    y, r = x, right
    if width is None:
        width = x.shape[1]
    for step, j in enumerate(order[:-1]):
        half = y.shape[0] // 2
        mine = (me >> j) & 1
        keep = lax.dynamic_slice(y, (mine * half, column), (half, width))
        send = lax.dynamic_slice(y, ((1 - mine) * half, column), (half, width))
        r = lax.dynamic_slice(r, (mine * half, column), (half, width))
        column = 0
        got = lax.ppermute(send, axis, [(i, i ^ (1 << j)) for i in range(n)])
        if step == 1 and riders is not None:
            got, riders = lax.optimization_barrier((got, riders))
        y = keep + got
        if step == 0 and hold is not None:
            y, held = lax.optimization_barrier((y, hold[0]))
            riders = (hold[1](held), riders)
    top = order[-1]
    y = y + lax.ppermute(y, axis, [(i, i ^ (1 << top)) for i in range(n)])
    y = r - y
    for j in reversed(order[:-1]):
        mine = (me >> j) & 1
        got = lax.ppermute(y, axis, [(i, i ^ (1 << j)) for i in range(n)])
        low = jnp.where(mine == 0, y, got)
        high = jnp.where(mine == 0, got, y)
        y = jnp.concatenate([low, high], 0)
    return y, riders


def make_shards(n, m):
    power_of_two = n > 1 and (n & (n - 1)) == 0
    rhs_power_of_two = m > 1 and (m & (m - 1)) == 0

    def sum_scatter(x, riders=None):
        if power_of_two and n >= 4:
            return halving_sum_scatter(x, "blk", n, riders)
        return lax.psum_scatter(x, "blk", scatter_dimension=0, tiled=True), riders

    def gather(x):
        if power_of_two:
            return doubling_gather(x, "blk", n)
        return lax.all_gather(x, "blk", axis=0, tiled=True)

    def shards(factor_panel, solved_before, right_side, diag_inverse, coupling):
        if rhs_power_of_two:
            inverse_pieces = doubling_gather(diag_inverse[None], "rhs", m)
        else:
            inverse_pieces = lax.all_gather(diag_inverse, "rhs", axis=0)
        own_count = diag_inverse.shape[1]
        my_index = lax.axis_index("blk")

        def own_slice(matrix):
            return lax.dynamic_slice_in_dim(matrix, my_index * own_count, own_count, 0)

        first_sum = product(factor_panel[0], solved_before)
        first_sum, inverse_pieces = lax.optimization_barrier((first_sum, inverse_pieces))
        chained = power_of_two and n >= 4
        if not chained:
            panel_sum = product(factor_panel[1], solved_before)
        if chained:
            k = n.bit_length() - 1
            orders = (list(range(k)), [0, 2, 1] + list(range(3, k)) if k >= 3 else list(range(k)))
            width = first_sum.shape[1] // 2
            columns = (slice(0, width), slice(width, 2 * width))
            first_blocks = []
            for chain, (order, cols) in enumerate(zip(orders, columns)):
                remains, got_riders = ordered_reduce_then_gather(
                    first_sum, right_side[0], "blk", n, order,
                    inverse_pieces if chain == 0 else None,
                    (solved_before, lambda held: product(factor_panel[1], held)) if chain == 0 else None,
                    width, cols.start,
                )
                if chain == 0:
                    panel_sum, inverse_pieces = got_riders
                first_blocks.append(remains)
            inverse_full = jnp.concatenate(list(inverse_pieces), axis=2)
            first_blocks = [product(inverse_full[0], remains) for remains in first_blocks]
            second_blocks = []
            for order, cols, block in zip(orders, columns, first_blocks):
                remains, _ = ordered_reduce_then_gather(
                    panel_sum[:, cols] + product(coupling, block), right_side[1][:, cols], "blk", n, order
                )
                second_blocks.append(product(inverse_full[1], remains))
            first_block = jnp.concatenate(first_blocks, 1)
            second_block = jnp.concatenate(second_blocks, 1)
        else:
            inverse_full = jnp.concatenate(list(inverse_pieces), axis=2)
            first_part, panel_sum = sum_scatter(first_sum, panel_sum)
            first_remains = gather(own_slice(right_side[0]) - first_part)
            first_block = product(inverse_full[0], first_remains)
            second_part, _ = sum_scatter(panel_sum + product(coupling, first_block))
            second_remains = gather(own_slice(right_side[1]) - second_part)
            second_block = product(inverse_full[1], second_remains)
        return jnp.stack([first_block, second_block])

    return shards


def solution(mesh):
    placed = (
        P(None, None, "blk"),
        P("blk", "rhs"),
        P(None, None, "rhs"),
        P(None, "blk", "rhs"),
        P(None, "blk"),
    )
    return jax.shard_map(
        make_shards(mesh.shape["blk"], mesh.shape["rhs"]), mesh=mesh, in_specs=placed, out_specs=P(None, "blk", "rhs"), check_vma=False
    )
```

```python
import jax
import jax.numpy as jnp
from jax import lax
from jax.sharding import PartitionSpec as P


def product(left, right):
    return jnp.dot(left, right, precision=lax.Precision.HIGHEST, preferred_element_type=jnp.float32)


def halving_sum_scatter(x, axis, n, riders=None):
    k = n.bit_length() - 1
    me = lax.axis_index(axis)
    rows = x.shape[0] // n
    y = x.reshape((2,) * k + (rows,) + x.shape[1:])
    for j in range(k):
        bit_axis = k - 1 - j
        mine = (me >> j) & 1
        keep = lax.dynamic_index_in_dim(y, mine, bit_axis, keepdims=False)
        send = lax.dynamic_index_in_dim(y, 1 - mine, bit_axis, keepdims=False)
        got = lax.ppermute(send, axis, [(i, i ^ (1 << j)) for i in range(n)])
        if j == 1 and riders is not None:
            got, riders = lax.optimization_barrier((got, riders))
        y = keep + got
    return y.reshape((rows,) + x.shape[1:]), riders


def doubling_gather(x, axis, n):
    k = n.bit_length() - 1
    me = lax.axis_index(axis)
    y = x[None]
    for j in reversed(range(k)):
        mine = (me >> j) & 1
        got = lax.ppermute(y, axis, [(i, i ^ (1 << j)) for i in range(n)])
        low = jnp.where(mine == 0, y, got)
        high = jnp.where(mine == 0, got, y)
        y = jnp.stack([low, high], 1).reshape((-1,) + x.shape)
    return y.reshape((-1,) + x.shape[1:])


def reduce_then_gather(x, right, axis, n, riders=None):
    k = n.bit_length() - 1
    me = lax.axis_index(axis)
    rows = x.shape[0] // n
    y = x.reshape((2,) * k + (rows,) + x.shape[1:])
    r = right.reshape(y.shape)
    for j in range(k - 1):
        bit_axis = k - 1 - j
        mine = (me >> j) & 1
        keep = lax.dynamic_index_in_dim(y, mine, bit_axis, keepdims=False)
        send = lax.dynamic_index_in_dim(y, 1 - mine, bit_axis, keepdims=False)
        r = lax.dynamic_index_in_dim(r, mine, bit_axis, keepdims=False)
        got = lax.ppermute(send, axis, [(i, i ^ (1 << j)) for i in range(n)])
        if j == 1 and riders is not None:
            got, riders = lax.optimization_barrier((got, riders))
        y = keep + got
    top = k - 1
    y = y + lax.ppermute(y, axis, [(i, i ^ (1 << top)) for i in range(n)])
    y = r - y
    for j in reversed(range(k - 1)):
        mine = (me >> j) & 1
        got = lax.ppermute(y, axis, [(i, i ^ (1 << j)) for i in range(n)])
        low = jnp.where(mine == 0, y, got)
        high = jnp.where(mine == 0, got, y)
        y = jnp.stack([low, high], k - 1 - j)
    return y.reshape(x.shape), riders


def ordered_reduce_then_gather(x, right, axis, n, order, riders=None, hold=None):
    me = lax.axis_index(axis)
    y, r = x, right
    for step, j in enumerate(order[:-1]):
        half = y.shape[0] // 2
        mine = (me >> j) & 1
        keep = lax.dynamic_slice_in_dim(y, mine * half, half, 0)
        send = lax.dynamic_slice_in_dim(y, (1 - mine) * half, half, 0)
        r = lax.dynamic_slice_in_dim(r, mine * half, half, 0)
        got = lax.ppermute(send, axis, [(i, i ^ (1 << j)) for i in range(n)])
        if step == 1 and riders is not None:
            got, riders = lax.optimization_barrier((got, riders))
        y = keep + got
        if step == 0 and hold is not None:
            y, held = lax.optimization_barrier((y, hold[0]))
            riders = (hold[1](held), riders)
    top = order[-1]
    y = y + lax.ppermute(y, axis, [(i, i ^ (1 << top)) for i in range(n)])
    y = r - y
    for j in reversed(order[:-1]):
        mine = (me >> j) & 1
        got = lax.ppermute(y, axis, [(i, i ^ (1 << j)) for i in range(n)])
        low = jnp.where(mine == 0, y, got)
        high = jnp.where(mine == 0, got, y)
        y = jnp.concatenate([low, high], 0)
    return y, riders


def make_shards(n, m):
    power_of_two = n > 1 and (n & (n - 1)) == 0
    rhs_power_of_two = m > 1 and (m & (m - 1)) == 0

    def sum_scatter(x, riders=None):
        if power_of_two and n >= 4:
            return halving_sum_scatter(x, "blk", n, riders)
        return lax.psum_scatter(x, "blk", scatter_dimension=0, tiled=True), riders

    def gather(x):
        if power_of_two:
            return doubling_gather(x, "blk", n)
        return lax.all_gather(x, "blk", axis=0, tiled=True)

    def shards(factor_panel, solved_before, right_side, diag_inverse, coupling):
        if rhs_power_of_two:
            inverse_pieces = doubling_gather(diag_inverse[None], "rhs", m)
        else:
            inverse_pieces = lax.all_gather(diag_inverse, "rhs", axis=0)
        own_count = diag_inverse.shape[1]
        my_index = lax.axis_index("blk")

        def own_slice(matrix):
            return lax.dynamic_slice_in_dim(matrix, my_index * own_count, own_count, 0)

        chained = power_of_two and n >= 4
        if chained:
            width = solved_before.shape[1] // 2
            first_sums = [product(factor_panel[0], solved_before[:, :width])]
            second_input, inverse_pieces = lax.optimization_barrier((first_sums[0], (solved_before, inverse_pieces)))[1]
            first_sums.append(product(factor_panel[0], second_input[:, width:]))
        else:
            first_sum = product(factor_panel[0], solved_before)
            first_sum, inverse_pieces = lax.optimization_barrier((first_sum, inverse_pieces))
        if not chained:
            panel_sum = product(factor_panel[1], solved_before)
        if chained:
            k = n.bit_length() - 1
            orders = (list(range(k)), [0, 2, 1] + list(range(3, k)) if k >= 3 else list(range(k)))
            columns = (slice(0, width), slice(width, 2 * width))
            first_blocks = []
            for chain, (order, cols) in enumerate(zip(orders, columns)):
                remains, got_riders = ordered_reduce_then_gather(
                    first_sums[chain], right_side[0][:, cols], "blk", n, order,
                    inverse_pieces if chain == 0 else None,
                    (solved_before, lambda held: product(factor_panel[1], held)) if chain == 0 else None,
                )
                if chain == 0:
                    panel_sum, inverse_pieces = got_riders
                first_blocks.append(remains)
            inverse_full = jnp.concatenate(list(inverse_pieces), axis=2)
            first_blocks = [product(inverse_full[0], remains) for remains in first_blocks]
            second_blocks = []
            for order, cols, block in zip(orders, columns, first_blocks):
                remains, _ = ordered_reduce_then_gather(
                    panel_sum[:, cols] + product(coupling, block), right_side[1][:, cols], "blk", n, order
                )
                second_blocks.append(product(inverse_full[1], remains))
            first_block = jnp.concatenate(first_blocks, 1)
            second_block = jnp.concatenate(second_blocks, 1)
        else:
            inverse_full = jnp.concatenate(list(inverse_pieces), axis=2)
            first_part, panel_sum = sum_scatter(first_sum, panel_sum)
            first_remains = gather(own_slice(right_side[0]) - first_part)
            first_block = product(inverse_full[0], first_remains)
            second_part, _ = sum_scatter(panel_sum + product(coupling, first_block))
            second_remains = gather(own_slice(right_side[1]) - second_part)
            second_block = product(inverse_full[1], second_remains)
        return jnp.stack([first_block, second_block])

    return shards


def solution(mesh):
    placed = (
        P(None, None, "blk"),
        P("blk", "rhs"),
        P(None, None, "rhs"),
        P(None, "blk", "rhs"),
        P(None, "blk"),
    )
    return jax.shard_map(
        make_shards(mesh.shape["blk"], mesh.shape["rhs"]), mesh=mesh, in_specs=placed, out_specs=P(None, "blk", "rhs"), check_vma=False
    )
```

```python
import jax
import jax.numpy as jnp
from jax import lax
from jax.sharding import PartitionSpec as P


def product(left, right):
    return jnp.dot(left, right, precision=lax.Precision.HIGHEST, preferred_element_type=jnp.float32)


def halving_sum_scatter(x, axis, n, riders=None):
    k = n.bit_length() - 1
    me = lax.axis_index(axis)
    rows = x.shape[0] // n
    y = x.reshape((2,) * k + (rows,) + x.shape[1:])
    for j in range(k):
        bit_axis = k - 1 - j
        mine = (me >> j) & 1
        keep = lax.dynamic_index_in_dim(y, mine, bit_axis, keepdims=False)
        send = lax.dynamic_index_in_dim(y, 1 - mine, bit_axis, keepdims=False)
        got = lax.ppermute(send, axis, [(i, i ^ (1 << j)) for i in range(n)])
        if j == 1 and riders is not None:
            got, riders = lax.optimization_barrier((got, riders))
        y = keep + got
    return y.reshape((rows,) + x.shape[1:]), riders


def doubling_gather(x, axis, n):
    k = n.bit_length() - 1
    me = lax.axis_index(axis)
    y = x[None]
    for j in reversed(range(k)):
        mine = (me >> j) & 1
        got = lax.ppermute(y, axis, [(i, i ^ (1 << j)) for i in range(n)])
        low = jnp.where(mine == 0, y, got)
        high = jnp.where(mine == 0, got, y)
        y = jnp.stack([low, high], 1).reshape((-1,) + x.shape)
    return y.reshape((-1,) + x.shape[1:])


def reduce_then_gather(x, right, axis, n, riders=None):
    k = n.bit_length() - 1
    me = lax.axis_index(axis)
    rows = x.shape[0] // n
    y = x.reshape((2,) * k + (rows,) + x.shape[1:])
    r = right.reshape(y.shape)
    for j in range(k - 1):
        bit_axis = k - 1 - j
        mine = (me >> j) & 1
        keep = lax.dynamic_index_in_dim(y, mine, bit_axis, keepdims=False)
        send = lax.dynamic_index_in_dim(y, 1 - mine, bit_axis, keepdims=False)
        r = lax.dynamic_index_in_dim(r, mine, bit_axis, keepdims=False)
        got = lax.ppermute(send, axis, [(i, i ^ (1 << j)) for i in range(n)])
        if j == 1 and riders is not None:
            got, riders = lax.optimization_barrier((got, riders))
        y = keep + got
    top = k - 1
    y = y + lax.ppermute(y, axis, [(i, i ^ (1 << top)) for i in range(n)])
    y = r - y
    for j in reversed(range(k - 1)):
        mine = (me >> j) & 1
        got = lax.ppermute(y, axis, [(i, i ^ (1 << j)) for i in range(n)])
        low = jnp.where(mine == 0, y, got)
        high = jnp.where(mine == 0, got, y)
        y = jnp.stack([low, high], k - 1 - j)
    return y.reshape(x.shape), riders


def ordered_reduce_then_gather(x, right, axis, n, order, riders=None, hold=None, width=None, column=0):
    me = lax.axis_index(axis)
    y, r = x, right
    if width is None:
        width = x.shape[1]
    for step, j in enumerate(order[:-1]):
        half = y.shape[0] // 2
        mine = (me >> j) & 1
        keep = lax.dynamic_slice(y, (mine * half, column), (half, width))
        send = lax.dynamic_slice(y, ((1 - mine) * half, column), (half, width))
        r = lax.dynamic_slice(r, (mine * half, column), (half, width))
        column = 0
        got = lax.ppermute(send, axis, [(i, i ^ (1 << j)) for i in range(n)])
        if step == 1 and riders is not None:
            got, riders = lax.optimization_barrier((got, riders))
        y = keep + got
        if step == 0 and hold is not None:
            y, held = lax.optimization_barrier((y, hold[0]))
            riders = (hold[1](held), riders)
    top = order[-1]
    y = y + lax.ppermute(y, axis, [(i, i ^ (1 << top)) for i in range(n)])
    y = r - y
    for j in reversed(order[:-1]):
        mine = (me >> j) & 1
        got = lax.ppermute(y, axis, [(i, i ^ (1 << j)) for i in range(n)])
        low = jnp.where(mine == 0, y, got)
        high = jnp.where(mine == 0, got, y)
        y = jnp.concatenate([low, high], 0)
    return y, riders


def make_shards(n, m):
    power_of_two = n > 1 and (n & (n - 1)) == 0
    rhs_power_of_two = m > 1 and (m & (m - 1)) == 0

    def sum_scatter(x, riders=None):
        if power_of_two and n >= 4:
            return halving_sum_scatter(x, "blk", n, riders)
        return lax.psum_scatter(x, "blk", scatter_dimension=0, tiled=True), riders

    def gather(x):
        if power_of_two:
            return doubling_gather(x, "blk", n)
        return lax.all_gather(x, "blk", axis=0, tiled=True)

    def shards(factor_panel, solved_before, right_side, diag_inverse, coupling):
        if rhs_power_of_two:
            inverse_pieces = doubling_gather(diag_inverse[None], "rhs", m)
        else:
            inverse_pieces = lax.all_gather(diag_inverse, "rhs", axis=0)
        own_count = diag_inverse.shape[1]
        my_index = lax.axis_index("blk")

        def own_slice(matrix):
            return lax.dynamic_slice_in_dim(matrix, my_index * own_count, own_count, 0)

        first_sum = product(factor_panel[0], solved_before)
        first_sum, inverse_pieces = lax.optimization_barrier((first_sum, inverse_pieces))
        chained = power_of_two and n >= 4
        if not chained:
            panel_sum = product(factor_panel[1], solved_before)
        if chained:
            k = n.bit_length() - 1
            orders = (list(range(k)), [0, 2, 1] + list(range(3, k)) if k >= 3 else list(range(k)))
            width = first_sum.shape[1] // 2
            columns = (slice(0, width), slice(width, 2 * width))
            first_blocks = []
            for chain, (order, cols) in enumerate(zip(orders, columns)):
                remains, got_riders = ordered_reduce_then_gather(
                    first_sum if chain == 0 else first_sum[:, cols], right_side[0] if chain == 0 else right_side[0][:, cols],
                    "blk", n, order,
                    inverse_pieces if chain == 0 else None,
                    (solved_before, lambda held: product(factor_panel[1], held)) if chain == 0 else None,
                    width if chain == 0 else None,
                )
                if chain == 0:
                    panel_sum, inverse_pieces = got_riders
                first_blocks.append(remains)
            inverse_full = jnp.concatenate(list(inverse_pieces), axis=2)
            first_blocks = [product(inverse_full[0], remains) for remains in first_blocks]
            second_blocks = []
            for order, cols, block in zip(orders, columns, first_blocks):
                remains, _ = ordered_reduce_then_gather(
                    panel_sum[:, cols] + product(coupling, block), right_side[1][:, cols], "blk", n, order
                )
                second_blocks.append(product(inverse_full[1], remains))
            first_block = jnp.concatenate(first_blocks, 1)
            second_block = jnp.concatenate(second_blocks, 1)
        else:
            inverse_full = jnp.concatenate(list(inverse_pieces), axis=2)
            first_part, panel_sum = sum_scatter(first_sum, panel_sum)
            first_remains = gather(own_slice(right_side[0]) - first_part)
            first_block = product(inverse_full[0], first_remains)
            second_part, _ = sum_scatter(panel_sum + product(coupling, first_block))
            second_remains = gather(own_slice(right_side[1]) - second_part)
            second_block = product(inverse_full[1], second_remains)
        return jnp.stack([first_block, second_block])

    return shards


def solution(mesh):
    placed = (
        P(None, None, "blk"),
        P("blk", "rhs"),
        P(None, None, "rhs"),
        P(None, "blk", "rhs"),
        P(None, "blk"),
    )
    return jax.shard_map(
        make_shards(mesh.shape["blk"], mesh.shape["rhs"]), mesh=mesh, in_specs=placed, out_specs=P(None, "blk", "rhs"), check_vma=False
    )
```

```python
import jax
import jax.numpy as jnp
from jax import lax
from jax.sharding import PartitionSpec as P


def product(left, right):
    return jnp.dot(left, right, precision=lax.Precision.HIGHEST, preferred_element_type=jnp.float32)


def halving_sum_scatter(x, axis, n, riders=None):
    k = n.bit_length() - 1
    me = lax.axis_index(axis)
    rows = x.shape[0] // n
    y = x.reshape((2,) * k + (rows,) + x.shape[1:])
    for j in range(k):
        bit_axis = k - 1 - j
        mine = (me >> j) & 1
        keep = lax.dynamic_index_in_dim(y, mine, bit_axis, keepdims=False)
        send = lax.dynamic_index_in_dim(y, 1 - mine, bit_axis, keepdims=False)
        got = lax.ppermute(send, axis, [(i, i ^ (1 << j)) for i in range(n)])
        if j == 1 and riders is not None:
            got, riders = lax.optimization_barrier((got, riders))
        y = keep + got
    return y.reshape((rows,) + x.shape[1:]), riders


def doubling_gather(x, axis, n):
    k = n.bit_length() - 1
    me = lax.axis_index(axis)
    y = x[None]
    for j in reversed(range(k)):
        mine = (me >> j) & 1
        got = lax.ppermute(y, axis, [(i, i ^ (1 << j)) for i in range(n)])
        low = jnp.where(mine == 0, y, got)
        high = jnp.where(mine == 0, got, y)
        y = jnp.stack([low, high], 1).reshape((-1,) + x.shape)
    return y.reshape((-1,) + x.shape[1:])


def reduce_then_gather(x, right, axis, n, riders=None):
    k = n.bit_length() - 1
    me = lax.axis_index(axis)
    rows = x.shape[0] // n
    y = x.reshape((2,) * k + (rows,) + x.shape[1:])
    r = right.reshape(y.shape)
    for j in range(k - 1):
        bit_axis = k - 1 - j
        mine = (me >> j) & 1
        keep = lax.dynamic_index_in_dim(y, mine, bit_axis, keepdims=False)
        send = lax.dynamic_index_in_dim(y, 1 - mine, bit_axis, keepdims=False)
        r = lax.dynamic_index_in_dim(r, mine, bit_axis, keepdims=False)
        got = lax.ppermute(send, axis, [(i, i ^ (1 << j)) for i in range(n)])
        if j == 1 and riders is not None:
            got, riders = lax.optimization_barrier((got, riders))
        y = keep + got
    top = k - 1
    y = y + lax.ppermute(y, axis, [(i, i ^ (1 << top)) for i in range(n)])
    y = r - y
    for j in reversed(range(k - 1)):
        mine = (me >> j) & 1
        got = lax.ppermute(y, axis, [(i, i ^ (1 << j)) for i in range(n)])
        low = jnp.where(mine == 0, y, got)
        high = jnp.where(mine == 0, got, y)
        y = jnp.stack([low, high], k - 1 - j)
    return y.reshape(x.shape), riders


def ordered_reduce_then_gather(x, right, axis, n, order, riders=None, hold=None):
    me = lax.axis_index(axis)
    y, r = x, right
    for step, j in enumerate(order[:-1]):
        half = y.shape[0] // 2
        mine = (me >> j) & 1
        keep = lax.dynamic_slice_in_dim(y, mine * half, half, 0)
        send = lax.dynamic_slice_in_dim(y, (1 - mine) * half, half, 0)
        r = lax.dynamic_slice_in_dim(r, mine * half, half, 0)
        got = lax.ppermute(send, axis, [(i, i ^ (1 << j)) for i in range(n)])
        if step == 1 and riders is not None:
            got, riders = lax.optimization_barrier((got, riders))
        y = keep + got
        if step == 0 and hold is not None:
            y, held = lax.optimization_barrier((y, hold[0]))
            riders = (hold[1](held), riders)
    top = order[-1]
    y = y + lax.ppermute(y, axis, [(i, i ^ (1 << top)) for i in range(n)])
    y = r - y
    for j in reversed(order[:-1]):
        mine = (me >> j) & 1
        got = lax.ppermute(y, axis, [(i, i ^ (1 << j)) for i in range(n)])
        low = jnp.where(mine == 0, y, got)
        high = jnp.where(mine == 0, got, y)
        y = jnp.concatenate([low, high], 0)
    return y, riders


def make_shards(n, m):
    power_of_two = n > 1 and (n & (n - 1)) == 0
    rhs_power_of_two = m > 1 and (m & (m - 1)) == 0

    def sum_scatter(x, riders=None):
        if power_of_two and n >= 4:
            return halving_sum_scatter(x, "blk", n, riders)
        return lax.psum_scatter(x, "blk", scatter_dimension=0, tiled=True), riders

    def gather(x):
        if power_of_two:
            return doubling_gather(x, "blk", n)
        return lax.all_gather(x, "blk", axis=0, tiled=True)

    def shards(factor_panel, solved_before, right_side, diag_inverse, coupling):
        own_count = diag_inverse.shape[1]
        my_index = lax.axis_index("blk")

        def own_slice(matrix):
            return lax.dynamic_slice_in_dim(matrix, my_index * own_count, own_count, 0)

        first_sum = product(factor_panel[0], solved_before)
        first_sum, held_inverse = lax.optimization_barrier((first_sum, diag_inverse))
        if rhs_power_of_two:
            inverse_pieces = doubling_gather(held_inverse[None], "rhs", m)
        else:
            inverse_pieces = lax.all_gather(held_inverse, "rhs", axis=0)
        chained = power_of_two and n >= 4
        if not chained:
            panel_sum = product(factor_panel[1], solved_before)
        if chained:
            k = n.bit_length() - 1
            orders = (list(range(k)), [0, 2, 1] + list(range(3, k)) if k >= 3 else list(range(k)))
            width = first_sum.shape[1] // 2
            columns = (slice(0, width), slice(width, 2 * width))
            first_blocks = []
            for chain, (order, cols) in enumerate(zip(orders, columns)):
                remains, got_riders = ordered_reduce_then_gather(
                    first_sum[:, cols], right_side[0][:, cols], "blk", n, order,
                    inverse_pieces if chain == 0 else None,
                    (solved_before, lambda held: product(factor_panel[1], held)) if chain == 0 else None,
                )
                if chain == 0:
                    panel_sum, inverse_pieces = got_riders
                first_blocks.append(remains)
            inverse_full = jnp.concatenate(list(inverse_pieces), axis=2)
            first_blocks = [product(inverse_full[0], remains) for remains in first_blocks]
            second_blocks = []
            for order, cols, block in zip(orders, columns, first_blocks):
                remains, _ = ordered_reduce_then_gather(
                    panel_sum[:, cols] + product(coupling, block), right_side[1][:, cols], "blk", n, order
                )
                second_blocks.append(product(inverse_full[1], remains))
            first_block = jnp.concatenate(first_blocks, 1)
            second_block = jnp.concatenate(second_blocks, 1)
        else:
            inverse_full = jnp.concatenate(list(inverse_pieces), axis=2)
            first_part, panel_sum = sum_scatter(first_sum, panel_sum)
            first_remains = gather(own_slice(right_side[0]) - first_part)
            first_block = product(inverse_full[0], first_remains)
            second_part, _ = sum_scatter(panel_sum + product(coupling, first_block))
            second_remains = gather(own_slice(right_side[1]) - second_part)
            second_block = product(inverse_full[1], second_remains)
        return jnp.stack([first_block, second_block])

    return shards


def solution(mesh):
    placed = (
        P(None, None, "blk"),
        P("blk", "rhs"),
        P(None, None, "rhs"),
        P(None, "blk", "rhs"),
        P(None, "blk"),
    )
    return jax.shard_map(
        make_shards(mesh.shape["blk"], mesh.shape["rhs"]), mesh=mesh, in_specs=placed, out_specs=P(None, "blk", "rhs"), check_vma=False
    )
```

```python
import jax
import jax.numpy as jnp
from jax import lax
from jax.sharding import PartitionSpec as P


def product(left, right):
    return jnp.dot(left, right, precision=lax.Precision.HIGHEST, preferred_element_type=jnp.float32)


def halving_sum_scatter(x, axis, n, riders=None):
    k = n.bit_length() - 1
    me = lax.axis_index(axis)
    rows = x.shape[0] // n
    y = x.reshape((2,) * k + (rows,) + x.shape[1:])
    for j in range(k):
        bit_axis = k - 1 - j
        mine = (me >> j) & 1
        keep = lax.dynamic_index_in_dim(y, mine, bit_axis, keepdims=False)
        send = lax.dynamic_index_in_dim(y, 1 - mine, bit_axis, keepdims=False)
        got = lax.ppermute(send, axis, [(i, i ^ (1 << j)) for i in range(n)])
        if j == 1 and riders is not None:
            got, riders = lax.optimization_barrier((got, riders))
        y = keep + got
    return y.reshape((rows,) + x.shape[1:]), riders


def doubling_gather(x, axis, n):
    k = n.bit_length() - 1
    me = lax.axis_index(axis)
    y = x[None]
    for j in reversed(range(k)):
        mine = (me >> j) & 1
        got = lax.ppermute(y, axis, [(i, i ^ (1 << j)) for i in range(n)])
        low = jnp.where(mine == 0, y, got)
        high = jnp.where(mine == 0, got, y)
        y = jnp.stack([low, high], 1).reshape((-1,) + x.shape)
    return y.reshape((-1,) + x.shape[1:])


def reduce_then_gather(x, right, axis, n, riders=None):
    k = n.bit_length() - 1
    me = lax.axis_index(axis)
    rows = x.shape[0] // n
    y = x.reshape((2,) * k + (rows,) + x.shape[1:])
    r = right.reshape(y.shape)
    for j in range(k - 1):
        bit_axis = k - 1 - j
        mine = (me >> j) & 1
        keep = lax.dynamic_index_in_dim(y, mine, bit_axis, keepdims=False)
        send = lax.dynamic_index_in_dim(y, 1 - mine, bit_axis, keepdims=False)
        r = lax.dynamic_index_in_dim(r, mine, bit_axis, keepdims=False)
        got = lax.ppermute(send, axis, [(i, i ^ (1 << j)) for i in range(n)])
        if j == 1 and riders is not None:
            got, riders = lax.optimization_barrier((got, riders))
        y = keep + got
    top = k - 1
    y = y + lax.ppermute(y, axis, [(i, i ^ (1 << top)) for i in range(n)])
    y = r - y
    for j in reversed(range(k - 1)):
        mine = (me >> j) & 1
        got = lax.ppermute(y, axis, [(i, i ^ (1 << j)) for i in range(n)])
        low = jnp.where(mine == 0, y, got)
        high = jnp.where(mine == 0, got, y)
        y = jnp.stack([low, high], k - 1 - j)
    return y.reshape(x.shape), riders


def ordered_reduce_then_gather(x, right, axis, n, order, riders=None, hold=None):
    me = lax.axis_index(axis)
    y, r = x, right
    for step, j in enumerate(order[:-1]):
        half = y.shape[0] // 2
        mine = (me >> j) & 1
        keep = lax.dynamic_slice_in_dim(y, mine * half, half, 0)
        send = lax.dynamic_slice_in_dim(y, (1 - mine) * half, half, 0)
        r = lax.dynamic_slice_in_dim(r, mine * half, half, 0)
        got = lax.ppermute(send, axis, [(i, i ^ (1 << j)) for i in range(n)])
        if step == 1 and riders is not None:
            got, riders = lax.optimization_barrier((got, riders))
        y = keep + got
        if step == 0 and hold is not None:
            y, held = lax.optimization_barrier((y, hold[0]))
            riders = (hold[1](held), riders)
    top = order[-1]
    y = y + lax.ppermute(y, axis, [(i, i ^ (1 << top)) for i in range(n)])
    y = r - y
    for j in reversed(order[:-1]):
        mine = (me >> j) & 1
        got = lax.ppermute(y, axis, [(i, i ^ (1 << j)) for i in range(n)])
        low = jnp.where(mine == 0, y, got)
        high = jnp.where(mine == 0, got, y)
        y = jnp.concatenate([low, high], 0)
    return y, riders


def paired_reduce_then_gather(xs, rights, axis, n, orders, riders=None, hold=None):
    me = lax.axis_index(axis)
    core_pairs = [(i, i ^ 1) for i in range(n)]
    mine = me & 1
    half = xs[0].shape[0] // 2
    keeps = [lax.dynamic_slice_in_dim(x, mine * half, half, 0) for x in xs]
    sends = [lax.dynamic_slice_in_dim(x, (1 - mine) * half, half, 0) for x in xs]
    rs = [lax.dynamic_slice_in_dim(r, mine * half, half, 0) for r in rights]
    got = lax.ppermute(jnp.stack(sends), axis, core_pairs)
    ys = [keeps[c] + got[c] for c in range(2)]
    if hold is not None:
        ys[0], held = lax.optimization_barrier((ys[0], hold[0]))
        riders = (hold[1](held), riders)
    for c in range(2):
        y, r = ys[c], rs[c]
        order = orders[c]
        for step, j in enumerate(order[1:-1], start=1):
            half = y.shape[0] // 2
            bit = (me >> j) & 1
            keep = lax.dynamic_slice_in_dim(y, bit * half, half, 0)
            send = lax.dynamic_slice_in_dim(y, (1 - bit) * half, half, 0)
            r = lax.dynamic_slice_in_dim(r, bit * half, half, 0)
            got = lax.ppermute(send, axis, [(i, i ^ (1 << j)) for i in range(n)])
            if step == 1 and c == 0 and riders is not None:
                got, riders = lax.optimization_barrier((got, riders))
            y = keep + got
        top = order[-1]
        y = y + lax.ppermute(y, axis, [(i, i ^ (1 << top)) for i in range(n)])
        y = r - y
        for j in reversed(order[1:-1]):
            bit = (me >> j) & 1
            got = lax.ppermute(y, axis, [(i, i ^ (1 << j)) for i in range(n)])
            y = jnp.concatenate([jnp.where(bit == 0, y, got), jnp.where(bit == 0, got, y)], 0)
        ys[c] = y
    got = lax.ppermute(jnp.stack(ys), axis, core_pairs)
    outs = [
        jnp.concatenate([jnp.where(mine == 0, ys[c], got[c]), jnp.where(mine == 0, got[c], ys[c])], 0) for c in range(2)
    ]
    return outs, riders


def make_shards(n, m):
    power_of_two = n > 1 and (n & (n - 1)) == 0
    rhs_power_of_two = m > 1 and (m & (m - 1)) == 0

    def sum_scatter(x, riders=None):
        if power_of_two and n >= 4:
            return halving_sum_scatter(x, "blk", n, riders)
        return lax.psum_scatter(x, "blk", scatter_dimension=0, tiled=True), riders

    def gather(x):
        if power_of_two:
            return doubling_gather(x, "blk", n)
        return lax.all_gather(x, "blk", axis=0, tiled=True)

    def shards(factor_panel, solved_before, right_side, diag_inverse, coupling):
        if rhs_power_of_two:
            inverse_pieces = doubling_gather(diag_inverse[None], "rhs", m)
        else:
            inverse_pieces = lax.all_gather(diag_inverse, "rhs", axis=0)
        own_count = diag_inverse.shape[1]
        my_index = lax.axis_index("blk")

        def own_slice(matrix):
            return lax.dynamic_slice_in_dim(matrix, my_index * own_count, own_count, 0)

        first_sum = product(factor_panel[0], solved_before)
        first_sum, inverse_pieces = lax.optimization_barrier((first_sum, inverse_pieces))
        chained = power_of_two and n >= 4
        if not chained:
            panel_sum = product(factor_panel[1], solved_before)
        if chained:
            k = n.bit_length() - 1
            orders = (list(range(k)), [0, 2, 1] + list(range(3, k)) if k >= 3 else list(range(k)))
            width = first_sum.shape[1] // 2
            columns = (slice(0, width), slice(width, 2 * width))
            first_remains, (panel_sum, inverse_pieces) = paired_reduce_then_gather(
                [first_sum[:, cols] for cols in columns], [right_side[0][:, cols] for cols in columns], "blk", n, orders,
                inverse_pieces, (solved_before, lambda held: product(factor_panel[1], held)),
            )
            inverse_full = jnp.concatenate(list(inverse_pieces), axis=2)
            first_blocks = [product(inverse_full[0], remains) for remains in first_remains]
            second_remains, _ = paired_reduce_then_gather(
                [panel_sum[:, cols] + product(coupling, block) for cols, block in zip(columns, first_blocks)],
                [right_side[1][:, cols] for cols in columns], "blk", n, orders,
            )
            second_blocks = [product(inverse_full[1], remains) for remains in second_remains]
            first_block = jnp.concatenate(first_blocks, 1)
            second_block = jnp.concatenate(second_blocks, 1)
        else:
            inverse_full = jnp.concatenate(list(inverse_pieces), axis=2)
            first_part, panel_sum = sum_scatter(first_sum, panel_sum)
            first_remains = gather(own_slice(right_side[0]) - first_part)
            first_block = product(inverse_full[0], first_remains)
            second_part, _ = sum_scatter(panel_sum + product(coupling, first_block))
            second_remains = gather(own_slice(right_side[1]) - second_part)
            second_block = product(inverse_full[1], second_remains)
        return jnp.stack([first_block, second_block])

    return shards


def solution(mesh):
    placed = (
        P(None, None, "blk"),
        P("blk", "rhs"),
        P(None, None, "rhs"),
        P(None, "blk", "rhs"),
        P(None, "blk"),
    )
    return jax.shard_map(
        make_shards(mesh.shape["blk"], mesh.shape["rhs"]), mesh=mesh, in_specs=placed, out_specs=P(None, "blk", "rhs"), check_vma=False
    )
```

```python
import jax
import jax.numpy as jnp
from jax import lax
from jax.sharding import PartitionSpec as P


def product(left, right):
    return jnp.dot(left, right, precision=lax.Precision.HIGHEST, preferred_element_type=jnp.float32)


def halving_sum_scatter(x, axis, n, riders=None):
    k = n.bit_length() - 1
    me = lax.axis_index(axis)
    rows = x.shape[0] // n
    y = x.reshape((2,) * k + (rows,) + x.shape[1:])
    for j in range(k):
        bit_axis = k - 1 - j
        mine = (me >> j) & 1
        keep = lax.dynamic_index_in_dim(y, mine, bit_axis, keepdims=False)
        send = lax.dynamic_index_in_dim(y, 1 - mine, bit_axis, keepdims=False)
        got = lax.ppermute(send, axis, [(i, i ^ (1 << j)) for i in range(n)])
        if j == 1 and riders is not None:
            got, riders = lax.optimization_barrier((got, riders))
        y = keep + got
    return y.reshape((rows,) + x.shape[1:]), riders


def doubling_gather(x, axis, n):
    k = n.bit_length() - 1
    me = lax.axis_index(axis)
    y = x[None]
    for j in reversed(range(k)):
        mine = (me >> j) & 1
        got = lax.ppermute(y, axis, [(i, i ^ (1 << j)) for i in range(n)])
        low = jnp.where(mine == 0, y, got)
        high = jnp.where(mine == 0, got, y)
        y = jnp.stack([low, high], 1).reshape((-1,) + x.shape)
    return y.reshape((-1,) + x.shape[1:])


def reduce_then_gather(x, right, axis, n, riders=None):
    k = n.bit_length() - 1
    me = lax.axis_index(axis)
    rows = x.shape[0] // n
    y = x.reshape((2,) * k + (rows,) + x.shape[1:])
    r = right.reshape(y.shape)
    for j in range(k - 1):
        bit_axis = k - 1 - j
        mine = (me >> j) & 1
        keep = lax.dynamic_index_in_dim(y, mine, bit_axis, keepdims=False)
        send = lax.dynamic_index_in_dim(y, 1 - mine, bit_axis, keepdims=False)
        r = lax.dynamic_index_in_dim(r, mine, bit_axis, keepdims=False)
        got = lax.ppermute(send, axis, [(i, i ^ (1 << j)) for i in range(n)])
        if j == 1 and riders is not None:
            got, riders = lax.optimization_barrier((got, riders))
        y = keep + got
    top = k - 1
    y = y + lax.ppermute(y, axis, [(i, i ^ (1 << top)) for i in range(n)])
    y = r - y
    for j in reversed(range(k - 1)):
        mine = (me >> j) & 1
        got = lax.ppermute(y, axis, [(i, i ^ (1 << j)) for i in range(n)])
        low = jnp.where(mine == 0, y, got)
        high = jnp.where(mine == 0, got, y)
        y = jnp.stack([low, high], k - 1 - j)
    return y.reshape(x.shape), riders


def ordered_reduce_then_gather(x, right, axis, n, order, riders=None, hold=None):
    me = lax.axis_index(axis)
    y, r = x, right
    for step, j in enumerate(order[:-1]):
        half = y.shape[0] // 2
        mine = (me >> j) & 1
        keep = lax.dynamic_slice_in_dim(y, mine * half, half, 0)
        send = lax.dynamic_slice_in_dim(y, (1 - mine) * half, half, 0)
        r = lax.dynamic_slice_in_dim(r, mine * half, half, 0)
        got = lax.ppermute(send, axis, [(i, i ^ (1 << j)) for i in range(n)])
        if step == 1 and riders is not None:
            got, riders = lax.optimization_barrier((got, riders))
        y = keep + got
        if step == 0 and hold is not None:
            y, held = lax.optimization_barrier((y, hold[0]))
            riders = (hold[1](held), riders)
    top = order[-1]
    y = y + lax.ppermute(y, axis, [(i, i ^ (1 << top)) for i in range(n)])
    y = r - y
    for j in reversed(order[:-1]):
        mine = (me >> j) & 1
        got = lax.ppermute(y, axis, [(i, i ^ (1 << j)) for i in range(n)])
        low = jnp.where(mine == 0, y, got)
        high = jnp.where(mine == 0, got, y)
        y = jnp.concatenate([low, high], 0)
    return y, riders


def make_shards(n, m):
    power_of_two = n > 1 and (n & (n - 1)) == 0
    rhs_power_of_two = m > 1 and (m & (m - 1)) == 0

    def sum_scatter(x, riders=None):
        if power_of_two and n >= 4:
            return halving_sum_scatter(x, "blk", n, riders)
        return lax.psum_scatter(x, "blk", scatter_dimension=0, tiled=True), riders

    def gather(x):
        if power_of_two:
            return doubling_gather(x, "blk", n)
        return lax.all_gather(x, "blk", axis=0, tiled=True)

    def shards(factor_panel, solved_before, right_side, diag_inverse, coupling):
        def gather_inverse(inverse):
            if rhs_power_of_two:
                return doubling_gather(inverse[None], "rhs", m)
            return lax.all_gather(inverse, "rhs", axis=0)

        own_count = diag_inverse.shape[1]
        my_index = lax.axis_index("blk")

        def own_slice(matrix):
            return lax.dynamic_slice_in_dim(matrix, my_index * own_count, own_count, 0)

        first_sum = product(factor_panel[0], solved_before)
        chained = power_of_two and n >= 4
        if not chained:
            inverse_pieces = gather_inverse(diag_inverse)
            first_sum, inverse_pieces = lax.optimization_barrier((first_sum, inverse_pieces))
            panel_sum = product(factor_panel[1], solved_before)
        if chained:
            k = n.bit_length() - 1
            orders = (list(range(k)), [0, 2, 1] + list(range(3, k)) if k >= 3 else list(range(k)))
            width = first_sum.shape[1] // 2
            columns = (slice(0, width), slice(width, 2 * width))
            first_blocks = []
            for chain, (order, cols) in enumerate(zip(orders, columns)):
                remains, got_riders = ordered_reduce_then_gather(
                    first_sum[:, cols], right_side[0][:, cols], "blk", n, order,
                    None,
                    ((solved_before, diag_inverse), lambda held: (product(factor_panel[1], held[0]), gather_inverse(held[1])))
                    if chain == 0 else None,
                )
                if chain == 0:
                    (panel_sum, inverse_pieces), _ = got_riders
                first_blocks.append(remains)
            inverse_full = jnp.concatenate(list(inverse_pieces), axis=2)
            first_blocks = [product(inverse_full[0], remains) for remains in first_blocks]
            second_blocks = []
            for order, cols, block in zip(orders, columns, first_blocks):
                remains, _ = ordered_reduce_then_gather(
                    panel_sum[:, cols] + product(coupling, block), right_side[1][:, cols], "blk", n, order
                )
                second_blocks.append(product(inverse_full[1], remains))
            first_block = jnp.concatenate(first_blocks, 1)
            second_block = jnp.concatenate(second_blocks, 1)
        else:
            inverse_full = jnp.concatenate(list(inverse_pieces), axis=2)
            first_part, panel_sum = sum_scatter(first_sum, panel_sum)
            first_remains = gather(own_slice(right_side[0]) - first_part)
            first_block = product(inverse_full[0], first_remains)
            second_part, _ = sum_scatter(panel_sum + product(coupling, first_block))
            second_remains = gather(own_slice(right_side[1]) - second_part)
            second_block = product(inverse_full[1], second_remains)
        return jnp.stack([first_block, second_block])

    return shards


def solution(mesh):
    placed = (
        P(None, None, "blk"),
        P("blk", "rhs"),
        P(None, None, "rhs"),
        P(None, "blk", "rhs"),
        P(None, "blk"),
    )
    return jax.shard_map(
        make_shards(mesh.shape["blk"], mesh.shape["rhs"]), mesh=mesh, in_specs=placed, out_specs=P(None, "blk", "rhs"), check_vma=False
    )
```

```python
import jax
import jax.numpy as jnp
from jax import lax
from jax.sharding import PartitionSpec as P


def product(left, right):
    return jnp.dot(left, right, precision=lax.Precision.HIGHEST, preferred_element_type=jnp.float32)


def halving_sum_scatter(x, axis, n, riders=None):
    k = n.bit_length() - 1
    me = lax.axis_index(axis)
    rows = x.shape[0] // n
    y = x.reshape((2,) * k + (rows,) + x.shape[1:])
    for j in range(k):
        bit_axis = k - 1 - j
        mine = (me >> j) & 1
        keep = lax.dynamic_index_in_dim(y, mine, bit_axis, keepdims=False)
        send = lax.dynamic_index_in_dim(y, 1 - mine, bit_axis, keepdims=False)
        got = lax.ppermute(send, axis, [(i, i ^ (1 << j)) for i in range(n)])
        if j == 1 and riders is not None:
            got, riders = lax.optimization_barrier((got, riders))
        y = keep + got
    return y.reshape((rows,) + x.shape[1:]), riders


def doubling_gather(x, axis, n):
    k = n.bit_length() - 1
    me = lax.axis_index(axis)
    y = x[None]
    for j in reversed(range(k)):
        mine = (me >> j) & 1
        got = lax.ppermute(y, axis, [(i, i ^ (1 << j)) for i in range(n)])
        low = jnp.where(mine == 0, y, got)
        high = jnp.where(mine == 0, got, y)
        y = jnp.stack([low, high], 1).reshape((-1,) + x.shape)
    return y.reshape((-1,) + x.shape[1:])


def reduce_then_gather(x, right, axis, n, riders=None):
    k = n.bit_length() - 1
    me = lax.axis_index(axis)
    rows = x.shape[0] // n
    y = x.reshape((2,) * k + (rows,) + x.shape[1:])
    r = right.reshape(y.shape)
    for j in range(k - 1):
        bit_axis = k - 1 - j
        mine = (me >> j) & 1
        keep = lax.dynamic_index_in_dim(y, mine, bit_axis, keepdims=False)
        send = lax.dynamic_index_in_dim(y, 1 - mine, bit_axis, keepdims=False)
        r = lax.dynamic_index_in_dim(r, mine, bit_axis, keepdims=False)
        got = lax.ppermute(send, axis, [(i, i ^ (1 << j)) for i in range(n)])
        if j == 1 and riders is not None:
            got, riders = lax.optimization_barrier((got, riders))
        y = keep + got
    top = k - 1
    y = y + lax.ppermute(y, axis, [(i, i ^ (1 << top)) for i in range(n)])
    y = r - y
    for j in reversed(range(k - 1)):
        mine = (me >> j) & 1
        got = lax.ppermute(y, axis, [(i, i ^ (1 << j)) for i in range(n)])
        low = jnp.where(mine == 0, y, got)
        high = jnp.where(mine == 0, got, y)
        y = jnp.stack([low, high], k - 1 - j)
    return y.reshape(x.shape), riders


def ordered_reduce_then_gather(x, right, axis, n, order, riders=None, hold=None):
    me = lax.axis_index(axis)
    y, r = x, right
    for step, j in enumerate(order[:-1]):
        half = y.shape[0] // 2
        mine = (me >> j) & 1
        keep = lax.dynamic_slice_in_dim(y, mine * half, half, 0)
        send = lax.dynamic_slice_in_dim(y, (1 - mine) * half, half, 0)
        r = lax.dynamic_slice_in_dim(r, mine * half, half, 0)
        got = lax.ppermute(send, axis, [(i, i ^ (1 << j)) for i in range(n)])
        if step == 1 and riders is not None:
            got, riders = lax.optimization_barrier((got, riders))
        y = keep + got
        if step == 0 and hold is not None:
            y, held = lax.optimization_barrier((y, hold[0]))
            riders = (hold[1](held), riders)
    top = order[-1]
    y = y + lax.ppermute(y, axis, [(i, i ^ (1 << top)) for i in range(n)])
    y = r - y
    for j in reversed(order[:-1]):
        mine = (me >> j) & 1
        got = lax.ppermute(y, axis, [(i, i ^ (1 << j)) for i in range(n)])
        low = jnp.where(mine == 0, y, got)
        high = jnp.where(mine == 0, got, y)
        y = jnp.concatenate([low, high], 0)
    return y, riders


def make_shards(n, m):
    power_of_two = n > 1 and (n & (n - 1)) == 0
    rhs_power_of_two = m > 1 and (m & (m - 1)) == 0

    def sum_scatter(x, riders=None):
        if power_of_two and n >= 4:
            return halving_sum_scatter(x, "blk", n, riders)
        return lax.psum_scatter(x, "blk", scatter_dimension=0, tiled=True), riders

    def gather(x):
        if power_of_two:
            return doubling_gather(x, "blk", n)
        return lax.all_gather(x, "blk", axis=0, tiled=True)

    def shards(factor_panel, solved_before, right_side, diag_inverse, coupling):
        if rhs_power_of_two:
            inverse_pieces = doubling_gather(diag_inverse[None], "rhs", m)
        else:
            inverse_pieces = lax.all_gather(diag_inverse, "rhs", axis=0)
        own_count = diag_inverse.shape[1]
        my_index = lax.axis_index("blk")

        def own_slice(matrix):
            return lax.dynamic_slice_in_dim(matrix, my_index * own_count, own_count, 0)

        first_sum = product(factor_panel[0], solved_before)
        first_sum, inverse_pieces = lax.optimization_barrier((first_sum, inverse_pieces))
        chained = power_of_two and n >= 4
        if not chained:
            panel_sum = product(factor_panel[1], solved_before)
        if chained:
            k = n.bit_length() - 1
            orders = (list(range(k)), [0, 2, 1] + list(range(3, k)) if k >= 3 else list(range(k)))
            width = first_sum.shape[1] // 2
            columns = (slice(0, width), slice(width, 2 * width))
            first_blocks = []
            for chain, (order, cols) in enumerate(zip(orders, columns)):
                remains, got_riders = ordered_reduce_then_gather(
                    first_sum[:, cols], right_side[0][:, cols], "blk", n, order,
                    inverse_pieces if chain == 1 else None,
                    (solved_before, lambda held: product(factor_panel[1], held)) if chain == 1 else None,
                )
                if chain == 1:
                    panel_sum, inverse_pieces = got_riders
                first_blocks.append(remains)
            inverse_full = jnp.concatenate(list(inverse_pieces), axis=2)
            first_blocks = [product(inverse_full[0], remains) for remains in first_blocks]
            second_blocks = []
            for order, cols, block in zip(orders, columns, first_blocks):
                remains, _ = ordered_reduce_then_gather(
                    panel_sum[:, cols] + product(coupling, block), right_side[1][:, cols], "blk", n, order
                )
                second_blocks.append(product(inverse_full[1], remains))
            first_block = jnp.concatenate(first_blocks, 1)
            second_block = jnp.concatenate(second_blocks, 1)
        else:
            inverse_full = jnp.concatenate(list(inverse_pieces), axis=2)
            first_part, panel_sum = sum_scatter(first_sum, panel_sum)
            first_remains = gather(own_slice(right_side[0]) - first_part)
            first_block = product(inverse_full[0], first_remains)
            second_part, _ = sum_scatter(panel_sum + product(coupling, first_block))
            second_remains = gather(own_slice(right_side[1]) - second_part)
            second_block = product(inverse_full[1], second_remains)
        return jnp.stack([first_block, second_block])

    return shards


def solution(mesh):
    placed = (
        P(None, None, "blk"),
        P("blk", "rhs"),
        P(None, None, "rhs"),
        P(None, "blk", "rhs"),
        P(None, "blk"),
    )
    return jax.shard_map(
        make_shards(mesh.shape["blk"], mesh.shape["rhs"]), mesh=mesh, in_specs=placed, out_specs=P(None, "blk", "rhs"), check_vma=False
    )
```

```python
import jax
import jax.numpy as jnp
from jax import lax
from jax.sharding import PartitionSpec as P


def product(left, right):
    return jnp.dot(left, right, precision=lax.Precision.HIGHEST, preferred_element_type=jnp.float32)


def halving_sum_scatter(x, axis, n, riders=None):
    k = n.bit_length() - 1
    me = lax.axis_index(axis)
    rows = x.shape[0] // n
    y = x.reshape((2,) * k + (rows,) + x.shape[1:])
    for j in range(k):
        bit_axis = k - 1 - j
        mine = (me >> j) & 1
        keep = lax.dynamic_index_in_dim(y, mine, bit_axis, keepdims=False)
        send = lax.dynamic_index_in_dim(y, 1 - mine, bit_axis, keepdims=False)
        got = lax.ppermute(send, axis, [(i, i ^ (1 << j)) for i in range(n)])
        if j == 1 and riders is not None:
            got, riders = lax.optimization_barrier((got, riders))
        y = keep + got
    return y.reshape((rows,) + x.shape[1:]), riders


def doubling_gather(x, axis, n):
    k = n.bit_length() - 1
    me = lax.axis_index(axis)
    y = x[None]
    for j in reversed(range(k)):
        mine = (me >> j) & 1
        got = lax.ppermute(y, axis, [(i, i ^ (1 << j)) for i in range(n)])
        low = jnp.where(mine == 0, y, got)
        high = jnp.where(mine == 0, got, y)
        y = jnp.stack([low, high], 1).reshape((-1,) + x.shape)
    return y.reshape((-1,) + x.shape[1:])


def reduce_then_gather(x, right, axis, n, riders=None):
    k = n.bit_length() - 1
    me = lax.axis_index(axis)
    rows = x.shape[0] // n
    y = x.reshape((2,) * k + (rows,) + x.shape[1:])
    r = right.reshape(y.shape)
    for j in range(k - 1):
        bit_axis = k - 1 - j
        mine = (me >> j) & 1
        keep = lax.dynamic_index_in_dim(y, mine, bit_axis, keepdims=False)
        send = lax.dynamic_index_in_dim(y, 1 - mine, bit_axis, keepdims=False)
        r = lax.dynamic_index_in_dim(r, mine, bit_axis, keepdims=False)
        got = lax.ppermute(send, axis, [(i, i ^ (1 << j)) for i in range(n)])
        if j == 1 and riders is not None:
            got, riders = lax.optimization_barrier((got, riders))
        y = keep + got
    top = k - 1
    y = y + lax.ppermute(y, axis, [(i, i ^ (1 << top)) for i in range(n)])
    y = r - y
    for j in reversed(range(k - 1)):
        mine = (me >> j) & 1
        got = lax.ppermute(y, axis, [(i, i ^ (1 << j)) for i in range(n)])
        low = jnp.where(mine == 0, y, got)
        high = jnp.where(mine == 0, got, y)
        y = jnp.stack([low, high], k - 1 - j)
    return y.reshape(x.shape), riders


def ordered_reduce_then_gather(x, right, axis, n, order, riders=None, hold=None):
    me = lax.axis_index(axis)
    y, r = x, right
    for step, j in enumerate(order[:-1]):
        half = y.shape[0] // 2
        mine = (me >> j) & 1
        keep = lax.dynamic_slice_in_dim(y, mine * half, half, 0)
        send = lax.dynamic_slice_in_dim(y, (1 - mine) * half, half, 0)
        r = lax.dynamic_slice_in_dim(r, mine * half, half, 0)
        got = lax.ppermute(send, axis, [(i, i ^ (1 << j)) for i in range(n)])
        if step == 1 and riders is not None:
            got, riders = lax.optimization_barrier((got, riders))
        y = keep + got
        if step == 0 and hold is not None:
            y, held = lax.optimization_barrier((y, hold[0]))
            riders = (hold[1](held), riders)
    top = order[-1]
    y = y + lax.ppermute(y, axis, [(i, i ^ (1 << top)) for i in range(n)])
    y = r - y
    for j in reversed(order[:-1]):
        mine = (me >> j) & 1
        got = lax.ppermute(y, axis, [(i, i ^ (1 << j)) for i in range(n)])
        low = jnp.where(mine == 0, y, got)
        high = jnp.where(mine == 0, got, y)
        y = jnp.concatenate([low, high], 0)
    return y, riders


def make_shards(n, m):
    power_of_two = n > 1 and (n & (n - 1)) == 0
    rhs_power_of_two = m > 1 and (m & (m - 1)) == 0

    def sum_scatter(x, riders=None):
        if power_of_two and n >= 4:
            return halving_sum_scatter(x, "blk", n, riders)
        return lax.psum_scatter(x, "blk", scatter_dimension=0, tiled=True), riders

    def gather(x):
        if power_of_two:
            return doubling_gather(x, "blk", n)
        return lax.all_gather(x, "blk", axis=0, tiled=True)

    def shards(factor_panel, solved_before, right_side, diag_inverse, coupling):
        if rhs_power_of_two:
            inverse_pieces = doubling_gather(diag_inverse[None], "rhs", m)
        else:
            inverse_pieces = lax.all_gather(diag_inverse, "rhs", axis=0)
        own_count = diag_inverse.shape[1]
        my_index = lax.axis_index("blk")

        def own_slice(matrix):
            return lax.dynamic_slice_in_dim(matrix, my_index * own_count, own_count, 0)

        first_sum = product(factor_panel[0], solved_before)
        first_sum, inverse_pieces = lax.optimization_barrier((first_sum, inverse_pieces))
        chained = power_of_two and n >= 4
        if not chained:
            panel_sum = product(factor_panel[1], solved_before)
        if chained:
            k = n.bit_length() - 1
            orders = (list(range(k)), [0, 2, 1] + list(range(3, k)) if k >= 3 else list(range(k)))
            width = first_sum.shape[1] // 2
            columns = (slice(0, width), slice(width, 2 * width))

            def column_halves(matrix):
                return tuple(matrix[:, cols] for cols in columns)

            first_blocks = []
            for chain, (order, cols) in enumerate(zip(orders, columns)):
                remains, got_riders = ordered_reduce_then_gather(
                    first_sum[:, cols], right_side[0][:, cols], "blk", n, order,
                    inverse_pieces if chain == 0 else None,
                    (solved_before, lambda held: column_halves(product(factor_panel[1], held))) if chain == 0 else None,
                )
                if chain == 0:
                    panel_sum, inverse_pieces = got_riders
                first_blocks.append(remains)
            inverse_full = jnp.concatenate(list(inverse_pieces), axis=2)
            first_blocks = [product(inverse_full[0], remains) for remains in first_blocks]
            second_blocks = []
            for chain, (order, cols, block) in enumerate(zip(orders, columns, first_blocks)):
                remains, _ = ordered_reduce_then_gather(
                    panel_sum[chain] + product(coupling, block), right_side[1][:, cols], "blk", n, order
                )
                second_blocks.append(product(inverse_full[1], remains))
            first_block = jnp.concatenate(first_blocks, 1)
            second_block = jnp.concatenate(second_blocks, 1)
        else:
            inverse_full = jnp.concatenate(list(inverse_pieces), axis=2)
            first_part, panel_sum = sum_scatter(first_sum, panel_sum)
            first_remains = gather(own_slice(right_side[0]) - first_part)
            first_block = product(inverse_full[0], first_remains)
            second_part, _ = sum_scatter(panel_sum + product(coupling, first_block))
            second_remains = gather(own_slice(right_side[1]) - second_part)
            second_block = product(inverse_full[1], second_remains)
        return jnp.stack([first_block, second_block])

    return shards


def solution(mesh):
    placed = (
        P(None, None, "blk"),
        P("blk", "rhs"),
        P(None, None, "rhs"),
        P(None, "blk", "rhs"),
        P(None, "blk"),
    )
    return jax.shard_map(
        make_shards(mesh.shape["blk"], mesh.shape["rhs"]), mesh=mesh, in_specs=placed, out_specs=P(None, "blk", "rhs"), check_vma=False
    )
```

```python
import jax
import jax.numpy as jnp
from jax import lax
from jax.sharding import PartitionSpec as P


def product(left, right):
    return jnp.dot(left, right, precision=lax.Precision.HIGHEST, preferred_element_type=jnp.float32)


def halving_sum_scatter(x, axis, n, riders=None):
    k = n.bit_length() - 1
    me = lax.axis_index(axis)
    rows = x.shape[0] // n
    y = x.reshape((2,) * k + (rows,) + x.shape[1:])
    for j in range(k):
        bit_axis = k - 1 - j
        mine = (me >> j) & 1
        keep = lax.dynamic_index_in_dim(y, mine, bit_axis, keepdims=False)
        send = lax.dynamic_index_in_dim(y, 1 - mine, bit_axis, keepdims=False)
        got = lax.ppermute(send, axis, [(i, i ^ (1 << j)) for i in range(n)])
        if j == 1 and riders is not None:
            got, riders = lax.optimization_barrier((got, riders))
        y = keep + got
    return y.reshape((rows,) + x.shape[1:]), riders


def doubling_gather(x, axis, n):
    k = n.bit_length() - 1
    me = lax.axis_index(axis)
    y = x[None]
    for j in reversed(range(k)):
        mine = (me >> j) & 1
        got = lax.ppermute(y, axis, [(i, i ^ (1 << j)) for i in range(n)])
        low = jnp.where(mine == 0, y, got)
        high = jnp.where(mine == 0, got, y)
        y = jnp.stack([low, high], 1).reshape((-1,) + x.shape)
    return y.reshape((-1,) + x.shape[1:])


def reduce_then_gather(x, right, axis, n, riders=None):
    k = n.bit_length() - 1
    me = lax.axis_index(axis)
    rows = x.shape[0] // n
    y = x.reshape((2,) * k + (rows,) + x.shape[1:])
    r = right.reshape(y.shape)
    for j in range(k - 1):
        bit_axis = k - 1 - j
        mine = (me >> j) & 1
        keep = lax.dynamic_index_in_dim(y, mine, bit_axis, keepdims=False)
        send = lax.dynamic_index_in_dim(y, 1 - mine, bit_axis, keepdims=False)
        r = lax.dynamic_index_in_dim(r, mine, bit_axis, keepdims=False)
        got = lax.ppermute(send, axis, [(i, i ^ (1 << j)) for i in range(n)])
        if j == 1 and riders is not None:
            got, riders = lax.optimization_barrier((got, riders))
        y = keep + got
    top = k - 1
    y = y + lax.ppermute(y, axis, [(i, i ^ (1 << top)) for i in range(n)])
    y = r - y
    for j in reversed(range(k - 1)):
        mine = (me >> j) & 1
        got = lax.ppermute(y, axis, [(i, i ^ (1 << j)) for i in range(n)])
        low = jnp.where(mine == 0, y, got)
        high = jnp.where(mine == 0, got, y)
        y = jnp.stack([low, high], k - 1 - j)
    return y.reshape(x.shape), riders


def ordered_reduce_then_gather(x, right, axis, n, order, riders=None, hold=None):
    me = lax.axis_index(axis)
    y, offset, held = x, 0, None
    for step, j in enumerate(order[:-1]):
        half = y.shape[0] // 2
        mine = (me >> j) & 1
        keep = lax.dynamic_slice_in_dim(y, mine * half, half, 0)
        send = lax.dynamic_slice_in_dim(y, (1 - mine) * half, half, 0)
        offset = offset + mine * half
        got = lax.ppermute(send, axis, [(i, i ^ (1 << j)) for i in range(n)])
        if step == 1 and riders is not None:
            got, riders = lax.optimization_barrier((got, riders))
        y = keep + got
        if step == 0 and hold is not None:
            y, held = lax.optimization_barrier((y, hold[0]))
            riders = (hold[1](held), riders)
    top = order[-1]
    y = y + lax.ppermute(y, axis, [(i, i ^ (1 << top)) for i in range(n)])
    if callable(right):
        right = right(held)
    y = lax.dynamic_slice_in_dim(right, offset, y.shape[0], 0) - y
    for j in reversed(order[:-1]):
        mine = (me >> j) & 1
        got = lax.ppermute(y, axis, [(i, i ^ (1 << j)) for i in range(n)])
        low = jnp.where(mine == 0, y, got)
        high = jnp.where(mine == 0, got, y)
        y = jnp.concatenate([low, high], 0)
    return y, riders


def make_shards(n, m):
    power_of_two = n > 1 and (n & (n - 1)) == 0
    rhs_power_of_two = m > 1 and (m & (m - 1)) == 0

    def sum_scatter(x, riders=None):
        if power_of_two and n >= 4:
            return halving_sum_scatter(x, "blk", n, riders)
        return lax.psum_scatter(x, "blk", scatter_dimension=0, tiled=True), riders

    def gather(x):
        if power_of_two:
            return doubling_gather(x, "blk", n)
        return lax.all_gather(x, "blk", axis=0, tiled=True)

    def shards(factor_panel, solved_before, right_side, diag_inverse, coupling):
        if rhs_power_of_two:
            inverse_pieces = doubling_gather(diag_inverse[None], "rhs", m)
        else:
            inverse_pieces = lax.all_gather(diag_inverse, "rhs", axis=0)
        own_count = diag_inverse.shape[1]
        my_index = lax.axis_index("blk")

        def own_slice(matrix):
            return lax.dynamic_slice_in_dim(matrix, my_index * own_count, own_count, 0)

        first_sum = product(factor_panel[0], solved_before)
        first_sum, inverse_pieces = lax.optimization_barrier((first_sum, inverse_pieces))
        chained = power_of_two and n >= 4
        if not chained:
            panel_sum = product(factor_panel[1], solved_before)
        if chained:
            k = n.bit_length() - 1
            orders = (list(range(k)), [0, 2, 1] + list(range(3, k)) if k >= 3 else list(range(k)))
            width = first_sum.shape[1] // 2
            columns = (slice(0, width), slice(width, 2 * width))

            def column_halves(matrix):
                return tuple(matrix[:, cols] for cols in columns)

            first_blocks = []
            for chain, (order, cols) in enumerate(zip(orders, columns)):
                if chain == 0:
                    remains, got_riders = ordered_reduce_then_gather(
                        first_sum[:, cols], lambda held, cols=cols: held[1][0][:, cols], "blk", n, order, inverse_pieces,
                        ((solved_before, right_side), lambda held: (column_halves(product(factor_panel[1], held[0])), held[1])),
                    )
                    (panel_sum, right_held), inverse_pieces = got_riders
                else:
                    remains, _ = ordered_reduce_then_gather(first_sum[:, cols], right_held[0][:, cols], "blk", n, order)
                first_blocks.append(remains)
            inverse_full = jnp.concatenate(list(inverse_pieces), axis=2)
            first_blocks = [product(inverse_full[0], remains) for remains in first_blocks]
            second_blocks = []
            for chain, (order, cols, block) in enumerate(zip(orders, columns, first_blocks)):
                remains, _ = ordered_reduce_then_gather(
                    panel_sum[chain] + product(coupling, block), right_held[1][:, cols], "blk", n, order
                )
                second_blocks.append(product(inverse_full[1], remains))
            first_block = jnp.concatenate(first_blocks, 1)
            second_block = jnp.concatenate(second_blocks, 1)
        else:
            inverse_full = jnp.concatenate(list(inverse_pieces), axis=2)
            first_part, panel_sum = sum_scatter(first_sum, panel_sum)
            first_remains = gather(own_slice(right_side[0]) - first_part)
            first_block = product(inverse_full[0], first_remains)
            second_part, _ = sum_scatter(panel_sum + product(coupling, first_block))
            second_remains = gather(own_slice(right_side[1]) - second_part)
            second_block = product(inverse_full[1], second_remains)
        return jnp.stack([first_block, second_block])

    return shards


def solution(mesh):
    placed = (
        P(None, None, "blk"),
        P("blk", "rhs"),
        P(None, None, "rhs"),
        P(None, "blk", "rhs"),
        P(None, "blk"),
    )
    return jax.shard_map(
        make_shards(mesh.shape["blk"], mesh.shape["rhs"]), mesh=mesh, in_specs=placed, out_specs=P(None, "blk", "rhs"), check_vma=False
    )
```

```python
import jax
import jax.numpy as jnp
from jax import lax
from jax.sharding import PartitionSpec as P


def product(left, right):
    return jnp.dot(left, right, precision=lax.Precision.HIGHEST, preferred_element_type=jnp.float32)


def halving_sum_scatter(x, axis, n, riders=None):
    k = n.bit_length() - 1
    me = lax.axis_index(axis)
    rows = x.shape[0] // n
    y = x.reshape((2,) * k + (rows,) + x.shape[1:])
    for j in range(k):
        bit_axis = k - 1 - j
        mine = (me >> j) & 1
        keep = lax.dynamic_index_in_dim(y, mine, bit_axis, keepdims=False)
        send = lax.dynamic_index_in_dim(y, 1 - mine, bit_axis, keepdims=False)
        got = lax.ppermute(send, axis, [(i, i ^ (1 << j)) for i in range(n)])
        if j == 1 and riders is not None:
            got, riders = lax.optimization_barrier((got, riders))
        y = keep + got
    return y.reshape((rows,) + x.shape[1:]), riders


def doubling_gather(x, axis, n):
    k = n.bit_length() - 1
    me = lax.axis_index(axis)
    y = x[None]
    for j in reversed(range(k)):
        mine = (me >> j) & 1
        got = lax.ppermute(y, axis, [(i, i ^ (1 << j)) for i in range(n)])
        low = jnp.where(mine == 0, y, got)
        high = jnp.where(mine == 0, got, y)
        y = jnp.stack([low, high], 1).reshape((-1,) + x.shape)
    return y.reshape((-1,) + x.shape[1:])


def reduce_then_gather(x, right, axis, n, riders=None):
    k = n.bit_length() - 1
    me = lax.axis_index(axis)
    rows = x.shape[0] // n
    y = x.reshape((2,) * k + (rows,) + x.shape[1:])
    r = right.reshape(y.shape)
    for j in range(k - 1):
        bit_axis = k - 1 - j
        mine = (me >> j) & 1
        keep = lax.dynamic_index_in_dim(y, mine, bit_axis, keepdims=False)
        send = lax.dynamic_index_in_dim(y, 1 - mine, bit_axis, keepdims=False)
        r = lax.dynamic_index_in_dim(r, mine, bit_axis, keepdims=False)
        got = lax.ppermute(send, axis, [(i, i ^ (1 << j)) for i in range(n)])
        if j == 1 and riders is not None:
            got, riders = lax.optimization_barrier((got, riders))
        y = keep + got
    top = k - 1
    y = y + lax.ppermute(y, axis, [(i, i ^ (1 << top)) for i in range(n)])
    y = r - y
    for j in reversed(range(k - 1)):
        mine = (me >> j) & 1
        got = lax.ppermute(y, axis, [(i, i ^ (1 << j)) for i in range(n)])
        low = jnp.where(mine == 0, y, got)
        high = jnp.where(mine == 0, got, y)
        y = jnp.stack([low, high], k - 1 - j)
    return y.reshape(x.shape), riders


def ordered_reduce_then_gather(x, right, axis, n, order, riders=None, hold=None):
    me = lax.axis_index(axis)
    y, r = x, right
    for step, j in enumerate(order[:-1]):
        half = y.shape[0] // 2
        mine = (me >> j) & 1
        keep = lax.dynamic_slice_in_dim(y, mine * half, half, 0)
        send = lax.dynamic_slice_in_dim(y, (1 - mine) * half, half, 0)
        r = lax.dynamic_slice_in_dim(r, mine * half, half, 0)
        got = lax.ppermute(send, axis, [(i, i ^ (1 << j)) for i in range(n)])
        if step == 1 and riders is not None:
            got, riders = lax.optimization_barrier((got, riders))
        y = keep + got
        if step == 0 and hold is not None:
            y, held = lax.optimization_barrier((y, hold[0]))
            riders = (hold[1](held), riders)
    top = order[-1]
    y = y + lax.ppermute(y, axis, [(i, i ^ (1 << top)) for i in range(n)])
    y = r - y
    for j in reversed(order[:-1]):
        mine = (me >> j) & 1
        got = lax.ppermute(y, axis, [(i, i ^ (1 << j)) for i in range(n)])
        low = jnp.where(mine == 0, y, got)
        high = jnp.where(mine == 0, got, y)
        y = jnp.concatenate([low, high], 0)
    return y, riders


def make_shards(n, m):
    power_of_two = n > 1 and (n & (n - 1)) == 0
    rhs_power_of_two = m > 1 and (m & (m - 1)) == 0

    def sum_scatter(x, riders=None):
        if power_of_two and n >= 4:
            return halving_sum_scatter(x, "blk", n, riders)
        return lax.psum_scatter(x, "blk", scatter_dimension=0, tiled=True), riders

    def gather(x):
        if power_of_two:
            return doubling_gather(x, "blk", n)
        return lax.all_gather(x, "blk", axis=0, tiled=True)

    def shards(factor_panel, solved_before, right_side, diag_inverse, coupling):
        if rhs_power_of_two:
            inverse_pieces = doubling_gather(diag_inverse[None], "rhs", m)
        else:
            inverse_pieces = lax.all_gather(diag_inverse, "rhs", axis=0)
        own_count = diag_inverse.shape[1]
        my_index = lax.axis_index("blk")

        def own_slice(matrix):
            return lax.dynamic_slice_in_dim(matrix, my_index * own_count, own_count, 0)

        first_sum = product(factor_panel[0], solved_before)
        first_sum, inverse_pieces = lax.optimization_barrier((first_sum, inverse_pieces))
        chained = power_of_two and n >= 4
        if not chained:
            panel_sum = product(factor_panel[1], solved_before)
        if chained:
            k = n.bit_length() - 1
            orders = (list(range(k)), [0, 2, 1] + list(range(3, k)) if k >= 3 else list(range(k)))
            width = first_sum.shape[1] // 2
            columns = (slice(0, width), slice(width, 2 * width))

            def column_halves(matrix):
                return tuple(matrix[:, cols] for cols in columns)

            first_blocks = []
            for chain, (order, cols) in enumerate(zip(orders, columns)):
                remains, got_riders = ordered_reduce_then_gather(
                    first_sum[:, cols], right_side[0][:, cols], "blk", n, order,
                    inverse_pieces if chain == 0 else None,
                    (solved_before, lambda held: column_halves(product(factor_panel[1], held))) if chain == 0 else None,
                )
                if chain == 0:
                    panel_sum, inverse_pieces = got_riders
                first_blocks.append(remains)
            inverse_full = jnp.concatenate(list(inverse_pieces), axis=2)
            first_blocks = [product(inverse_full[0], remains) for remains in first_blocks]
            second_blocks = []
            for chain, (order, cols, block) in enumerate(zip(orders, columns, first_blocks)):
                remains, _ = ordered_reduce_then_gather(
                    panel_sum[chain] + product(coupling, block), right_side[1][:, cols], "blk", n, order
                )
                second_blocks.append(product(inverse_full[1], remains))
            return jnp.concatenate([jnp.stack(pair) for pair in zip(first_blocks, second_blocks)], 2)
        else:
            inverse_full = jnp.concatenate(list(inverse_pieces), axis=2)
            first_part, panel_sum = sum_scatter(first_sum, panel_sum)
            first_remains = gather(own_slice(right_side[0]) - first_part)
            first_block = product(inverse_full[0], first_remains)
            second_part, _ = sum_scatter(panel_sum + product(coupling, first_block))
            second_remains = gather(own_slice(right_side[1]) - second_part)
            second_block = product(inverse_full[1], second_remains)
        return jnp.stack([first_block, second_block])

    return shards


def solution(mesh):
    placed = (
        P(None, None, "blk"),
        P("blk", "rhs"),
        P(None, None, "rhs"),
        P(None, "blk", "rhs"),
        P(None, "blk"),
    )
    return jax.shard_map(
        make_shards(mesh.shape["blk"], mesh.shape["rhs"]), mesh=mesh, in_specs=placed, out_specs=P(None, "blk", "rhs"), check_vma=False
    )
```

```python
import jax
import jax.numpy as jnp
from jax import lax
from jax.sharding import PartitionSpec as P


def product(left, right):
    return jnp.dot(left, right, precision=lax.Precision.HIGHEST, preferred_element_type=jnp.float32)


def halving_sum_scatter(x, axis, n, riders=None):
    k = n.bit_length() - 1
    me = lax.axis_index(axis)
    rows = x.shape[0] // n
    y = x.reshape((2,) * k + (rows,) + x.shape[1:])
    for j in range(k):
        bit_axis = k - 1 - j
        mine = (me >> j) & 1
        keep = lax.dynamic_index_in_dim(y, mine, bit_axis, keepdims=False)
        send = lax.dynamic_index_in_dim(y, 1 - mine, bit_axis, keepdims=False)
        got = lax.ppermute(send, axis, [(i, i ^ (1 << j)) for i in range(n)])
        if j == 1 and riders is not None:
            got, riders = lax.optimization_barrier((got, riders))
        y = keep + got
    return y.reshape((rows,) + x.shape[1:]), riders


def doubling_gather(x, axis, n):
    k = n.bit_length() - 1
    me = lax.axis_index(axis)
    y = x[None]
    for j in reversed(range(k)):
        mine = (me >> j) & 1
        got = lax.ppermute(y, axis, [(i, i ^ (1 << j)) for i in range(n)])
        low = jnp.where(mine == 0, y, got)
        high = jnp.where(mine == 0, got, y)
        y = jnp.stack([low, high], 1).reshape((-1,) + x.shape)
    return y.reshape((-1,) + x.shape[1:])


def reduce_then_gather(x, right, axis, n, riders=None):
    k = n.bit_length() - 1
    me = lax.axis_index(axis)
    rows = x.shape[0] // n
    y = x.reshape((2,) * k + (rows,) + x.shape[1:])
    r = right.reshape(y.shape)
    for j in range(k - 1):
        bit_axis = k - 1 - j
        mine = (me >> j) & 1
        keep = lax.dynamic_index_in_dim(y, mine, bit_axis, keepdims=False)
        send = lax.dynamic_index_in_dim(y, 1 - mine, bit_axis, keepdims=False)
        r = lax.dynamic_index_in_dim(r, mine, bit_axis, keepdims=False)
        got = lax.ppermute(send, axis, [(i, i ^ (1 << j)) for i in range(n)])
        if j == 1 and riders is not None:
            got, riders = lax.optimization_barrier((got, riders))
        y = keep + got
    top = k - 1
    y = y + lax.ppermute(y, axis, [(i, i ^ (1 << top)) for i in range(n)])
    y = r - y
    for j in reversed(range(k - 1)):
        mine = (me >> j) & 1
        got = lax.ppermute(y, axis, [(i, i ^ (1 << j)) for i in range(n)])
        low = jnp.where(mine == 0, y, got)
        high = jnp.where(mine == 0, got, y)
        y = jnp.stack([low, high], k - 1 - j)
    return y.reshape(x.shape), riders


def ordered_reduce_then_gather(x, right, axis, n, order, riders=None, hold=None):
    me = lax.axis_index(axis)
    y, r = x, right
    for step, j in enumerate(order[:-1]):
        half = y.shape[0] // 2
        mine = (me >> j) & 1
        keep = lax.dynamic_slice_in_dim(y, mine * half, half, 0)
        send = lax.dynamic_slice_in_dim(y, (1 - mine) * half, half, 0)
        r = lax.dynamic_slice_in_dim(r, mine * half, half, 0)
        got = lax.ppermute(send, axis, [(i, i ^ (1 << j)) for i in range(n)])
        if step == 1 and riders is not None:
            got, riders = lax.optimization_barrier((got, riders))
        y = keep + got
        if step == 0 and hold is not None:
            y, held = lax.optimization_barrier((y, hold[0]))
            riders = (hold[1](held), riders)
    top = order[-1]
    y = y + lax.ppermute(y, axis, [(i, i ^ (1 << top)) for i in range(n)])
    y = r - y
    for j in reversed(order[:-1]):
        mine = (me >> j) & 1
        got = lax.ppermute(y, axis, [(i, i ^ (1 << j)) for i in range(n)])
        low = jnp.where(mine == 0, y, got)
        high = jnp.where(mine == 0, got, y)
        y = jnp.concatenate([low, high], 0)
    return y, riders


def make_shards(n, m):
    power_of_two = n > 1 and (n & (n - 1)) == 0
    rhs_power_of_two = m > 1 and (m & (m - 1)) == 0

    def sum_scatter(x, riders=None):
        if power_of_two and n >= 4:
            return halving_sum_scatter(x, "blk", n, riders)
        return lax.psum_scatter(x, "blk", scatter_dimension=0, tiled=True), riders

    def gather(x):
        if power_of_two:
            return doubling_gather(x, "blk", n)
        return lax.all_gather(x, "blk", axis=0, tiled=True)

    def shards(factor_panel, solved_before, right_side, diag_inverse, coupling):
        if rhs_power_of_two:
            inverse_pieces = doubling_gather(diag_inverse[None], "rhs", m)
        else:
            inverse_pieces = lax.all_gather(diag_inverse, "rhs", axis=0)
        own_count = diag_inverse.shape[1]
        my_index = lax.axis_index("blk")

        def own_slice(matrix):
            return lax.dynamic_slice_in_dim(matrix, my_index * own_count, own_count, 0)

        first_sum = product(factor_panel[0], solved_before)
        first_sum, inverse_pieces = lax.optimization_barrier((first_sum, inverse_pieces))
        chained = power_of_two and n >= 4
        if not chained:
            panel_sum = product(factor_panel[1], solved_before)
        if chained:
            k = n.bit_length() - 1
            orders = (list(range(k)), [0, 2, 1] + list(range(3, k)) if k >= 3 else list(range(k)))
            width = first_sum.shape[1] // 2
            columns = (slice(0, width), slice(width, 2 * width))

            def column_halves(matrix):
                return tuple(matrix[:, cols] for cols in columns)

            first_blocks = []
            for chain, (order, cols) in enumerate(zip(orders, columns)):
                remains, got_riders = ordered_reduce_then_gather(
                    first_sum[:, cols], right_side[0][:, cols], "blk", n, order,
                    inverse_pieces if chain == 0 else None,
                    (solved_before, lambda held: column_halves(product(factor_panel[1], held))) if chain == 0 else None,
                )
                if chain == 0:
                    panel_sum, inverse_pieces = got_riders
                first_blocks.append(remains)
            inverse_full = jnp.concatenate(list(inverse_pieces), axis=2)
            first_blocks = [product(inverse_full[0], remains) for remains in first_blocks]
            second_blocks = []
            for chain, (order, cols, block) in enumerate(zip(orders[::-1], columns, first_blocks)):
                remains, _ = ordered_reduce_then_gather(
                    panel_sum[chain] + product(coupling, block), right_side[1][:, cols], "blk", n, order
                )
                second_blocks.append(product(inverse_full[1], remains))
            first_block = jnp.concatenate(first_blocks, 1)
            second_block = jnp.concatenate(second_blocks, 1)
        else:
            inverse_full = jnp.concatenate(list(inverse_pieces), axis=2)
            first_part, panel_sum = sum_scatter(first_sum, panel_sum)
            first_remains = gather(own_slice(right_side[0]) - first_part)
            first_block = product(inverse_full[0], first_remains)
            second_part, _ = sum_scatter(panel_sum + product(coupling, first_block))
            second_remains = gather(own_slice(right_side[1]) - second_part)
            second_block = product(inverse_full[1], second_remains)
        return jnp.stack([first_block, second_block])

    return shards


def solution(mesh):
    placed = (
        P(None, None, "blk"),
        P("blk", "rhs"),
        P(None, None, "rhs"),
        P(None, "blk", "rhs"),
        P(None, "blk"),
    )
    return jax.shard_map(
        make_shards(mesh.shape["blk"], mesh.shape["rhs"]), mesh=mesh, in_specs=placed, out_specs=P(None, "blk", "rhs"), check_vma=False
    )
```

```python
import jax
import jax.numpy as jnp
from jax import lax
from jax.sharding import PartitionSpec as P


def product(left, right):
    return jnp.dot(left, right, precision=lax.Precision.HIGHEST, preferred_element_type=jnp.float32)


def halving_sum_scatter(x, axis, n, riders=None):
    k = n.bit_length() - 1
    me = lax.axis_index(axis)
    rows = x.shape[0] // n
    y = x.reshape((2,) * k + (rows,) + x.shape[1:])
    for j in range(k):
        bit_axis = k - 1 - j
        mine = (me >> j) & 1
        keep = lax.dynamic_index_in_dim(y, mine, bit_axis, keepdims=False)
        send = lax.dynamic_index_in_dim(y, 1 - mine, bit_axis, keepdims=False)
        got = lax.ppermute(send, axis, [(i, i ^ (1 << j)) for i in range(n)])
        if j == 1 and riders is not None:
            got, riders = lax.optimization_barrier((got, riders))
        y = keep + got
    return y.reshape((rows,) + x.shape[1:]), riders


def doubling_gather(x, axis, n):
    k = n.bit_length() - 1
    me = lax.axis_index(axis)
    y = x[None]
    for j in reversed(range(k)):
        mine = (me >> j) & 1
        got = lax.ppermute(y, axis, [(i, i ^ (1 << j)) for i in range(n)])
        low = jnp.where(mine == 0, y, got)
        high = jnp.where(mine == 0, got, y)
        y = jnp.stack([low, high], 1).reshape((-1,) + x.shape)
    return y.reshape((-1,) + x.shape[1:])


def reduce_then_gather(x, right, axis, n, riders=None):
    k = n.bit_length() - 1
    me = lax.axis_index(axis)
    rows = x.shape[0] // n
    y = x.reshape((2,) * k + (rows,) + x.shape[1:])
    r = right.reshape(y.shape)
    for j in range(k - 1):
        bit_axis = k - 1 - j
        mine = (me >> j) & 1
        keep = lax.dynamic_index_in_dim(y, mine, bit_axis, keepdims=False)
        send = lax.dynamic_index_in_dim(y, 1 - mine, bit_axis, keepdims=False)
        r = lax.dynamic_index_in_dim(r, mine, bit_axis, keepdims=False)
        got = lax.ppermute(send, axis, [(i, i ^ (1 << j)) for i in range(n)])
        if j == 1 and riders is not None:
            got, riders = lax.optimization_barrier((got, riders))
        y = keep + got
    top = k - 1
    y = y + lax.ppermute(y, axis, [(i, i ^ (1 << top)) for i in range(n)])
    y = r - y
    for j in reversed(range(k - 1)):
        mine = (me >> j) & 1
        got = lax.ppermute(y, axis, [(i, i ^ (1 << j)) for i in range(n)])
        low = jnp.where(mine == 0, y, got)
        high = jnp.where(mine == 0, got, y)
        y = jnp.stack([low, high], k - 1 - j)
    return y.reshape(x.shape), riders


def ordered_reduce_then_gather(x, right, axis, n, order, riders=None, hold=None):
    me = lax.axis_index(axis)
    y, r = x, right
    for step, j in enumerate(order[:-1]):
        half = y.shape[0] // 2
        mine = (me >> j) & 1
        keep = lax.dynamic_slice_in_dim(y, mine * half, half, 0)
        send = lax.dynamic_slice_in_dim(y, (1 - mine) * half, half, 0)
        r = lax.dynamic_slice_in_dim(r, mine * half, half, 0)
        got = lax.ppermute(send, axis, [(i, i ^ (1 << j)) for i in range(n)])
        if step == 1 and riders is not None:
            got, riders = lax.optimization_barrier((got, riders))
        y = keep + got
        if step == 0 and hold is not None:
            y, held = lax.optimization_barrier((y, hold[0]))
            riders = (hold[1](held), riders)
    top = order[-1]
    y = y + lax.ppermute(y, axis, [(i, i ^ (1 << top)) for i in range(n)])
    y = r - y
    for j in reversed(order[:-1]):
        mine = (me >> j) & 1
        got = lax.ppermute(y, axis, [(i, i ^ (1 << j)) for i in range(n)])
        low = jnp.where(mine == 0, y, got)
        high = jnp.where(mine == 0, got, y)
        y = jnp.concatenate([low, high], 0)
    return y, riders


def make_shards(n, m):
    power_of_two = n > 1 and (n & (n - 1)) == 0
    rhs_power_of_two = m > 1 and (m & (m - 1)) == 0

    def sum_scatter(x, riders=None):
        if power_of_two and n >= 4:
            return halving_sum_scatter(x, "blk", n, riders)
        return lax.psum_scatter(x, "blk", scatter_dimension=0, tiled=True), riders

    def gather(x):
        if power_of_two:
            return doubling_gather(x, "blk", n)
        return lax.all_gather(x, "blk", axis=0, tiled=True)

    def shards(factor_panel, solved_before, right_side, diag_inverse, coupling):
        if rhs_power_of_two:
            inverse_pieces = doubling_gather(diag_inverse[None], "rhs", m)
        else:
            inverse_pieces = lax.all_gather(diag_inverse, "rhs", axis=0)
        own_count = diag_inverse.shape[1]
        my_index = lax.axis_index("blk")

        def own_slice(matrix):
            return lax.dynamic_slice_in_dim(matrix, my_index * own_count, own_count, 0)

        first_sum = product(factor_panel[0], solved_before)
        first_sum, inverse_pieces = lax.optimization_barrier((first_sum, inverse_pieces))
        chained = power_of_two and n >= 4
        if not chained:
            panel_sum = product(factor_panel[1], solved_before)
        if chained:
            k = n.bit_length() - 1
            orders = (list(range(k)), [0, 2, 1] + list(range(3, k)) if k >= 3 else list(range(k)))
            width = first_sum.shape[1] // 2
            columns = (slice(0, width), slice(width, 2 * width))

            def column_halves(matrix):
                return tuple(matrix[:, cols] for cols in columns)

            first_blocks = []
            for chain, (order, cols) in enumerate(zip(orders, columns[::-1])):
                remains, got_riders = ordered_reduce_then_gather(
                    first_sum[:, cols], right_side[0][:, cols], "blk", n, order,
                    inverse_pieces if chain == 0 else None,
                    (solved_before, lambda held: column_halves(product(factor_panel[1], held))) if chain == 0 else None,
                )
                if chain == 0:
                    panel_sum, inverse_pieces = got_riders
                first_blocks.append(remains)
            inverse_full = jnp.concatenate(list(inverse_pieces), axis=2)
            first_blocks = [product(inverse_full[0], remains) for remains in first_blocks[::-1]]
            second_blocks = []
            for chain, (order, cols, block) in enumerate(zip(orders[::-1], columns, first_blocks)):
                remains, _ = ordered_reduce_then_gather(
                    panel_sum[chain] + product(coupling, block), right_side[1][:, cols], "blk", n, order
                )
                second_blocks.append(product(inverse_full[1], remains))
            first_block = jnp.concatenate(first_blocks, 1)
            second_block = jnp.concatenate(second_blocks, 1)
        else:
            inverse_full = jnp.concatenate(list(inverse_pieces), axis=2)
            first_part, panel_sum = sum_scatter(first_sum, panel_sum)
            first_remains = gather(own_slice(right_side[0]) - first_part)
            first_block = product(inverse_full[0], first_remains)
            second_part, _ = sum_scatter(panel_sum + product(coupling, first_block))
            second_remains = gather(own_slice(right_side[1]) - second_part)
            second_block = product(inverse_full[1], second_remains)
        return jnp.stack([first_block, second_block])

    return shards


def solution(mesh):
    placed = (
        P(None, None, "blk"),
        P("blk", "rhs"),
        P(None, None, "rhs"),
        P(None, "blk", "rhs"),
        P(None, "blk"),
    )
    return jax.shard_map(
        make_shards(mesh.shape["blk"], mesh.shape["rhs"]), mesh=mesh, in_specs=placed, out_specs=P(None, "blk", "rhs"), check_vma=False
    )
```

```python
import jax
import jax.numpy as jnp
from jax import lax
from jax.sharding import PartitionSpec as P


def product(left, right):
    return jnp.dot(left, right, precision=lax.Precision.HIGHEST, preferred_element_type=jnp.float32)


def halving_sum_scatter(x, axis, n, riders=None):
    k = n.bit_length() - 1
    me = lax.axis_index(axis)
    rows = x.shape[0] // n
    y = x.reshape((2,) * k + (rows,) + x.shape[1:])
    for j in range(k):
        bit_axis = k - 1 - j
        mine = (me >> j) & 1
        keep = lax.dynamic_index_in_dim(y, mine, bit_axis, keepdims=False)
        send = lax.dynamic_index_in_dim(y, 1 - mine, bit_axis, keepdims=False)
        got = lax.ppermute(send, axis, [(i, i ^ (1 << j)) for i in range(n)])
        if j == 1 and riders is not None:
            got, riders = lax.optimization_barrier((got, riders))
        y = keep + got
    return y.reshape((rows,) + x.shape[1:]), riders


def doubling_gather(x, axis, n):
    k = n.bit_length() - 1
    me = lax.axis_index(axis)
    y = x[None]
    for j in reversed(range(k)):
        mine = (me >> j) & 1
        got = lax.ppermute(y, axis, [(i, i ^ (1 << j)) for i in range(n)])
        low = jnp.where(mine == 0, y, got)
        high = jnp.where(mine == 0, got, y)
        y = jnp.stack([low, high], 1).reshape((-1,) + x.shape)
    return y.reshape((-1,) + x.shape[1:])


def reduce_then_gather(x, right, axis, n, riders=None):
    k = n.bit_length() - 1
    me = lax.axis_index(axis)
    rows = x.shape[0] // n
    y = x.reshape((2,) * k + (rows,) + x.shape[1:])
    r = right.reshape(y.shape)
    for j in range(k - 1):
        bit_axis = k - 1 - j
        mine = (me >> j) & 1
        keep = lax.dynamic_index_in_dim(y, mine, bit_axis, keepdims=False)
        send = lax.dynamic_index_in_dim(y, 1 - mine, bit_axis, keepdims=False)
        r = lax.dynamic_index_in_dim(r, mine, bit_axis, keepdims=False)
        got = lax.ppermute(send, axis, [(i, i ^ (1 << j)) for i in range(n)])
        if j == 1 and riders is not None:
            got, riders = lax.optimization_barrier((got, riders))
        y = keep + got
    top = k - 1
    y = y + lax.ppermute(y, axis, [(i, i ^ (1 << top)) for i in range(n)])
    y = r - y
    for j in reversed(range(k - 1)):
        mine = (me >> j) & 1
        got = lax.ppermute(y, axis, [(i, i ^ (1 << j)) for i in range(n)])
        low = jnp.where(mine == 0, y, got)
        high = jnp.where(mine == 0, got, y)
        y = jnp.stack([low, high], k - 1 - j)
    return y.reshape(x.shape), riders


def ordered_reduce_then_gather(x, right, axis, n, order, riders=None, hold=None):
    me = lax.axis_index(axis)
    y, r = x, right
    for step, j in enumerate(order[:-1]):
        half = y.shape[0] // 2
        mine = (me >> j) & 1
        keep = lax.dynamic_slice_in_dim(y, mine * half, half, 0)
        send = lax.dynamic_slice_in_dim(y, (1 - mine) * half, half, 0)
        r = lax.dynamic_slice_in_dim(r, mine * half, half, 0)
        got = lax.ppermute(send, axis, [(i, i ^ (1 << j)) for i in range(n)])
        if step == 1 and riders is not None:
            got, riders = lax.optimization_barrier((got, riders))
        y = keep + got
        if step == 0 and hold is not None:
            y, held = lax.optimization_barrier((y, hold[0]))
            riders = (hold[1](held), riders)
    top = order[-1]
    y = y + lax.ppermute(y, axis, [(i, i ^ (1 << top)) for i in range(n)])
    y = r - y
    for j in reversed(order[:-1]):
        mine = (me >> j) & 1
        got = lax.ppermute(y, axis, [(i, i ^ (1 << j)) for i in range(n)])
        low = jnp.where(mine == 0, y, got)
        high = jnp.where(mine == 0, got, y)
        y = jnp.concatenate([low, high], 0)
    return y, riders


def make_shards(n, m):
    power_of_two = n > 1 and (n & (n - 1)) == 0
    rhs_power_of_two = m > 1 and (m & (m - 1)) == 0

    def sum_scatter(x, riders=None):
        if power_of_two and n >= 4:
            return halving_sum_scatter(x, "blk", n, riders)
        return lax.psum_scatter(x, "blk", scatter_dimension=0, tiled=True), riders

    def gather(x):
        if power_of_two:
            return doubling_gather(x, "blk", n)
        return lax.all_gather(x, "blk", axis=0, tiled=True)

    def shards(factor_panel, solved_before, right_side, diag_inverse, coupling):
        if rhs_power_of_two:
            inverse_pieces = doubling_gather(diag_inverse[None], "rhs", m)
        else:
            inverse_pieces = lax.all_gather(diag_inverse, "rhs", axis=0)
        own_count = diag_inverse.shape[1]
        my_index = lax.axis_index("blk")

        def own_slice(matrix):
            return lax.dynamic_slice_in_dim(matrix, my_index * own_count, own_count, 0)

        first_sum = product(factor_panel[0], solved_before)
        first_sum, inverse_pieces = lax.optimization_barrier((first_sum, inverse_pieces))
        chained = power_of_two and n >= 4
        if not chained:
            panel_sum = product(factor_panel[1], solved_before)
        if chained:
            k = n.bit_length() - 1
            orders = (list(range(k)), [0, 2, 1] + list(range(3, k)) if k >= 3 else list(range(k)))
            width = first_sum.shape[1] // 2
            columns = (slice(0, width), slice(width, 2 * width))

            def column_halves(matrix):
                return tuple(matrix[:, cols] for cols in columns)

            first_blocks = []
            for chain, (order, cols) in enumerate(zip(orders, columns)):
                remains, got_riders = ordered_reduce_then_gather(
                    first_sum[:, cols], right_side[0][:, cols], "blk", n, order,
                    inverse_pieces if chain == 0 else None,
                    (solved_before, lambda held: column_halves(product(factor_panel[1], held))) if chain == 0 else None,
                )
                if chain == 0:
                    panel_sum, inverse_pieces = got_riders
                first_blocks.append(remains)
            inverse_full = jnp.concatenate(list(inverse_pieces), axis=2)
            first_blocks = [product(inverse_full[0], remains) for remains in first_blocks]
            second_blocks = []
            for chain, (order, cols, block) in enumerate(zip(orders[::-1], columns, first_blocks)):
                remains, _ = ordered_reduce_then_gather(
                    panel_sum[chain] + product(coupling, block), right_side[1][:, cols], "blk", n, order
                )
                second_blocks.append(product(inverse_full[1], remains))
            return jnp.concatenate([jnp.stack(pair) for pair in zip(first_blocks, second_blocks)], 2)
        else:
            inverse_full = jnp.concatenate(list(inverse_pieces), axis=2)
            first_part, panel_sum = sum_scatter(first_sum, panel_sum)
            first_remains = gather(own_slice(right_side[0]) - first_part)
            first_block = product(inverse_full[0], first_remains)
            second_part, _ = sum_scatter(panel_sum + product(coupling, first_block))
            second_remains = gather(own_slice(right_side[1]) - second_part)
            second_block = product(inverse_full[1], second_remains)
        return jnp.stack([first_block, second_block])

    return shards


def solution(mesh):
    placed = (
        P(None, None, "blk"),
        P("blk", "rhs"),
        P(None, None, "rhs"),
        P(None, "blk", "rhs"),
        P(None, "blk"),
    )
    return jax.shard_map(
        make_shards(mesh.shape["blk"], mesh.shape["rhs"]), mesh=mesh, in_specs=placed, out_specs=P(None, "blk", "rhs"), check_vma=False
    )
```
